256 devices in a mesh: row: 32 (over z, x), col: 8 (over y, core).
Axes of the slice: x: 4, y: 4, z: 8, core: 2. Of those that a mesh axis runs over, the one named last changes fastest.
Arguments:
- x_points: bfloat16 [32768, 64], P(('row', 'col')), may hold values from -6 to 6
- y_points: bfloat16 [65536, 64], P(('col', 'row')), may hold values from -6 to 6
- row_mass: bfloat16 [32768], P(('row', 'col')), may hold values from 1 to 30, as said below
- col_mass: bfloat16 [65536], P(('col', 'row')), may hold values from 1 to 30, as said below
- multipliers: bfloat16 [32768, 64], P(('row', 'col')), may hold values from -12 to 12
- col_potential: bfloat16 [65536], P(('col', 'row')), may hold values from -3 to 3
- basket: float32 [64], replicated, may hold values from 0.05 to 0.25
- damping: float32 [64], replicated, may hold values from 0.3 to 1.5
Outputs:
- row_potential: float32 [32768], P('row')
- col_potential_new: float32 [65536], P('col')
- multipliers_new: float32 [32768, 64], P(('row', 'col'))
The draws below stay inside these ranges and needn't reach their ends.
Inputs may be any that keep to these rules, and one draw needn't show every extreme that they name: `row_mass`: weights rise along the points' order by up to a factor of three. `col_mass`: weights rise along the points' order by up to a factor of three.
All inputs are finite; a program needn't handle non-finite values.
Results may differ from the reference program's by a relative error of at most 0.0012.
Values may be sent and summed in bfloat16 or wider, within the bound.
No kernel may reach another device: no remote copies, remote signals or barrier semaphores. Data moves between devices by JAX's collectives and lax.ppermute only.
A program may use at most 64 MiB of HBM per device.

```python
import math
import jax
import jax.numpy as jnp
from jax import lax

A = 64
NX = 32768
NY = 65536


def rising_weights(key, count):
    base = jax.random.uniform(key, (count,), jnp.float32)
    scale = jnp.exp(base * jnp.log(10.0))
    ramp = 1.0 + 2.0 * jnp.arange(count, dtype=jnp.float32) / (count - 1)
    return scale * ramp


def draw_row_mass(key, part):
    return rising_weights(jax.random.fold_in(key, 11), NX).astype(jnp.bfloat16)


def draw_col_mass(key, part):
    return rising_weights(jax.random.fold_in(key, 23), NY).astype(jnp.bfloat16)


def draw_multipliers(key, part):
    first_key = jax.random.fold_in(jax.random.fold_in(key, 37), 0)
    base = jax.random.truncated_normal(first_key, -4.0, 4.0, (NX, A), jnp.float32)
    scale = 0.1
    return (base * scale).astype(jnp.bfloat16)


def levels(stream_key, extent, shards, least, largest):
    level = 1.0
    for dim, blocks in shards:
        draws = jax.random.uniform(jax.random.fold_in(jax.random.fold_in(stream_key, 6), dim), (blocks,), jnp.float32, least / len(shards), largest / len(shards))
        level = level * jnp.repeat(jnp.exp(draws), extent[dim] // blocks).reshape((-1,) + (1,) * (len(extent) - 1 - dim))
    return level


def normal_values(stream_key, dims, deviation, bound, shards=(), kind=jnp.bfloat16):
    values = jax.random.normal(stream_key, dims, jnp.float32) * deviation
    if len(shards) > 0:
        values = levels(stream_key, dims, shards, -0.22, 0.18) * values
    return jnp.clip(values, min=-bound, max=bound).astype(kind)


def setup_inputs(seed: int = 0) -> dict:
    key_of = jax.random.split(jax.random.key(seed), 9)
    x_points = normal_values(key_of[0], (NX, A), 1.0, 6.0, ((0, 256),))
    y_points = normal_values(key_of[1], (NY, A), 1.0, 6.0, ((0, 256),))
    row_mass = draw_row_mass(jax.random.fold_in(key_of[8], 71), 0)
    col_mass = draw_col_mass(jax.random.fold_in(key_of[8], 71), 0)
    multipliers = draw_multipliers(jax.random.fold_in(key_of[8], 71), 0)
    col_potential = normal_values(key_of[5], (NY,), 0.5, 3.0, ((0, 256),))
    basket = jnp.clip(jax.random.uniform(key_of[6], (A,), jnp.float32, 0.05, 0.25), 0.05, 0.25)
    damping = jnp.clip(jnp.exp(jax.random.uniform(key_of[7], (A,), jnp.float32, math.log(0.3), math.log(1.5))), 0.3, 1.5)
    return {"x_points": x_points, "y_points": y_points, "row_mass": row_mass, "col_mass": col_mass, "multipliers": multipliers, "col_potential": col_potential, "basket": basket, "damping": damping}


EPS = 0.5
KAPPA = 0.5
RIDGE = 1.0


def prepare_rows(x_rows, mult_rows, basket):
    xf = x_rows.astype(jnp.float32)
    hf = mult_rows.astype(jnp.float32)
    width = xf.shape[1]
    query = hf + (2.0 * KAPPA / width) * xf
    row_term = -jnp.sum(hf * xf, axis=1) - (KAPPA / width) * jnp.sum(xf * xf, axis=1)
    row_basket = jnp.sum(xf * basket[None, :], axis=1)
    return query, row_term, row_basket


def prepare_cols(y_cols, basket):
    yf = y_cols.astype(jnp.float32)
    width = yf.shape[1]
    col_term = -(KAPPA / width) * jnp.sum(yf * yf, axis=1)
    col_basket = jnp.sum(yf * basket[None, :], axis=1)
    features = jnp.concatenate([yf, yf * yf], axis=1).astype(jnp.bfloat16)
    return yf, col_term, col_basket, features


def scores(query, row_term, row_basket, y_float, col_term, col_basket):
    dots = lax.dot_general(query, y_float, (((1,), (1,)), ((), ())), precision=lax.Precision.HIGHEST, preferred_element_type=jnp.float32)
    payoff = jax.nn.relu(col_basket[None, :] - row_basket[:, None])
    return (dots + row_term[:, None] + col_term[None, :] + payoff) / EPS


def reference(x_points, y_points, row_mass, col_mass, multipliers, col_potential, basket, damping):
    query, row_term, row_basket = prepare_rows(x_points, multipliers, basket)
    y_float, col_term, col_basket, features = prepare_cols(y_points, basket)
    row_weight = row_mass.astype(jnp.float32)
    col_weight = col_mass.astype(jnp.float32)
    log_mu = jnp.log(row_weight) - jnp.log(jnp.sum(row_weight))
    log_nu = jnp.log(col_weight) - jnp.log(jnp.sum(col_weight))
    block = min(128, NX)
    count = NX // block
    starts = jnp.arange(count, dtype=jnp.int32) * block
    gshift = col_potential.astype(jnp.float32) / EPS + log_nu

    def cut(arr, start):
        return lax.dynamic_slice_in_dim(arr, start.astype(jnp.int32), block, 0)

    def block_scores(start):
        return scores(cut(query, start), cut(row_term, start), cut(row_basket, start), y_float, col_term, col_basket)

    def row_pass(start):
        z = block_scores(start) + gshift[None, :]
        top = jnp.max(z, axis=1)
        total = jnp.sum(jnp.exp(z - top[:, None]), axis=1)
        return top + jnp.log(total)

    row_potential = -EPS * lax.map(row_pass, starts).reshape(NX)
    fshift = row_potential / EPS + log_mu

    def col_pass(start):
        z = block_scores(start) + cut(fshift, start)[:, None]
        top = jnp.max(z, axis=0)
        total = jnp.sum(jnp.exp(z - top[None, :]), axis=0)
        return top, total

    tops, totals = lax.map(col_pass, starts)
    top = jnp.max(tops, axis=0)
    total = jnp.sum(totals * jnp.exp(tops - top[None, :]), axis=0)
    col_potential_new = -EPS * (top + jnp.log(total))
    gq = col_potential_new / EPS + log_nu
    fq = row_potential / EPS

    def moment_pass(start):
        plan = jnp.exp(block_scores(start) + cut(fq, start)[:, None] + gq[None, :]).astype(jnp.bfloat16)
        both = jnp.dot(plan, features, preferred_element_type=jnp.float32)
        mass = jnp.sum(plan.astype(jnp.float32), axis=1)
        return both, mass

    both, mass = lax.map(moment_pass, starts)
    both = both.reshape(NX, 2 * A)
    mass = mass.reshape(NX)
    first = both[:, :A]
    second = both[:, A:]
    xf = x_points.astype(jnp.float32)
    grad = first - xf * mass[:, None]
    curv = (second - 2.0 * xf * first + xf * xf * mass[:, None]) / EPS + RIDGE
    multipliers_new = multipliers.astype(jnp.float32) - damping[None, :] * grad / curv
    return row_potential, col_potential_new, multipliers_new
```

```python
import jax
import jax.numpy as jnp
from jax import lax
from jax.sharding import PartitionSpec as P

EPS = 0.5
KAPPA = 0.5
RIDGE = 1.0


def merge_lse(parts):
    top = jnp.max(parts, axis=0)
    return top + jnp.log(jnp.sum(jnp.exp(parts - top[None, :]), axis=0))


def on_device(x_points, y_points, row_mass, col_mass, multipliers, col_potential, basket, damping):
    width = x_points.shape[1]
    share = x_points.shape[0]
    x_pack = jnp.concatenate([x_points, multipliers, row_mass[:, None]], axis=1)
    x_rows_pack = lax.all_gather(x_pack, "col", axis=0, tiled=True)
    x_rows = x_rows_pack[:, :width]
    mult_rows = x_rows_pack[:, width : 2 * width]
    mass_rows = x_rows_pack[:, 2 * width]
    ny = y_points.shape[0]
    own_rmass = jnp.zeros((ny,), jnp.bfloat16).at[:share].set(row_mass)
    y_pack = jnp.concatenate(
        [y_points, col_potential[:, None], col_mass[:, None], own_rmass[:, None]], axis=1
    )
    y_cols_pack = lax.all_gather(y_pack, "row", axis=0, tiled=True)
    y_cols = y_cols_pack[:, :width]
    pot_cols = y_cols_pack[:, width].astype(jnp.float32)
    mass_cols = y_cols_pack[:, width + 1].astype(jnp.float32)
    rmass_part = jnp.sum(y_cols_pack[:, width + 2].astype(jnp.float32))

    xf = x_rows.astype(jnp.float32)
    hf = mult_rows.astype(jnp.float32)
    yf = y_cols.astype(jnp.float32)
    row_term2 = 2.0 * (-jnp.sum(hf * xf, axis=1) - KAPPA / width * jnp.sum(xf * xf, axis=1))
    row_basket2 = 2.0 * jnp.sum(xf * basket[None, :], axis=1)
    col_term2 = 2.0 * (-(KAPPA / width) * jnp.sum(yf * yf, axis=1))
    col_basket2 = 2.0 * jnp.sum(yf * basket[None, :], axis=1)
    q_aug = jnp.concatenate([mult_rows * 2, x_rows * (2.0 * KAPPA / width * 2.0)], axis=1)
    y_aug = jnp.concatenate([y_cols, y_cols], axis=1)
    features = jnp.concatenate([yf, yf * yf], axis=1).astype(jnp.bfloat16)

    row_weight = mass_rows.astype(jnp.float32)
    log_row = jnp.log(row_weight)
    log_col = jnp.log(mass_cols)
    nrows = x_rows.shape[0]
    block = min(128, nrows)
    count = nrows // block
    starts = jnp.arange(count, dtype=jnp.int32) * block

    def cut(arr, start):
        return lax.dynamic_slice_in_dim(arr, start, block, 0)

    def block_z(start, row_bias, col_bias):
        dots = jnp.dot(cut(q_aug, start), y_aug.T, preferred_element_type=jnp.float32)
        payoff = jnp.maximum(col_basket2[None, :] - cut(row_basket2, start)[:, None], 0.0)
        return dots + cut(row_bias, start)[:, None] + col_bias[None, :] + payoff

    gshift = col_term2 + pot_cols / EPS + log_col
    zero_rows = jnp.zeros((nrows,), jnp.float32)

    def row_pass(start):
        z = block_z(start, row_term2, gshift)
        top = jnp.max(z, axis=1)
        total = jnp.sum(jnp.exp(z - top[:, None]), axis=1)
        return top + jnp.log(total)

    row_local = lax.map(row_pass, starts).reshape(nrows)
    nu_part = jnp.sum(mass_cols)
    row_msg = jnp.concatenate([row_local, jnp.stack([nu_part, rmass_part])])
    row_all = lax.all_gather(row_msg, "col", axis=0)
    nu_total = jnp.sum(row_all[:, nrows])
    mu_total = jnp.sum(row_all[:, nrows + 1])
    log_nu_total = jnp.log(nu_total)
    row_potential = -EPS * (merge_lse(row_all[:, :nrows]) - log_nu_total)
    fshift = row_term2 + row_potential / EPS + log_row
    zero_cols = jnp.zeros_like(gshift)

    def col_pass(start):
        z = block_z(start, fshift, col_term2)
        top = jnp.max(z, axis=0)
        total = jnp.sum(jnp.exp(z - top[None, :]), axis=0)
        return (top, total)

    col_tops, col_totals = lax.map(col_pass, starts)
    col_top = jnp.max(col_tops, axis=0)
    col_total = jnp.sum(col_totals * jnp.exp(col_tops - col_top[None, :]), axis=0)
    col_local = col_top + jnp.log(col_total)
    col_all = lax.all_gather(col_local, "row", axis=0)
    col_potential_new = -EPS * (merge_lse(col_all) - jnp.log(mu_total))
    gq = col_term2 + col_potential_new / EPS + log_col - log_nu_total
    fq = row_term2 + row_potential / EPS

    def moment_pass(start):
        plan = jnp.exp(block_z(start, fq, gq)).astype(jnp.bfloat16)
        both = jnp.dot(plan, features, preferred_element_type=jnp.float32)
        mass = jnp.sum(plan.astype(jnp.float32), axis=1)
        return jnp.concatenate([both, mass[:, None]], axis=1)

    both = lax.map(moment_pass, starts).reshape(nrows, 2 * width + 1)
    own = lax.psum_scatter(both, "col", scatter_dimension=0, tiled=True)
    first = own[:, :width]
    second = own[:, width : 2 * width]
    own_mass = own[:, 2 * width]
    xo = x_points.astype(jnp.float32)
    grad = first - xo * own_mass[:, None]
    curv = (second - 2.0 * xo * first + xo * xo * own_mass[:, None]) / EPS + RIDGE
    multipliers_new = multipliers.astype(jnp.float32) - damping[None, :] * grad / curv
    return (row_potential, col_potential_new, multipliers_new)


def solution(mesh):
    placed = (
        P(("row", "col"), None),
        P(("col", "row"), None),
        P(("row", "col")),
        P(("col", "row")),
        P(("row", "col"), None),
        P(("col", "row")),
        P(),
        P(),
    )
    return jax.shard_map(
        on_device,
        mesh=mesh,
        in_specs=placed,
        out_specs=(P("row"), P("col"), P(("row", "col"), None)),
        check_vma=False,
    )
```

```python
import functools

import jax
import jax.numpy as jnp
from jax import lax
from jax.experimental import pallas as pl
from jax.sharding import Mesh, PartitionSpec as P

EPS = 0.5
KAPPA = 0.5
RIDGE = 1.0


ROW = ("z", "x")
COL = ("y", "core")


def gather_row(value):
    inner = lax.all_gather(value, ROW[1], axis=0, tiled=True)
    return lax.all_gather(inner, ROW[0], axis=0, tiled=True)


def gather_col(value):
    return lax.all_gather(value, COL, axis=0, tiled=True)


KF = 256
INTERPRET = False


def _row_lse_kernel(qa_ref, yat_ref, rb_ref, cb_ref, ra_ref, ca_ref, out_ref, *, tn):
    tm = qa_ref.shape[0]
    n = yat_ref.shape[1]
    qa = qa_ref[...]
    rb = rb_ref[...]
    ra = ra_ref[...]

    def body(k, carry):
        m, l = carry
        j = pl.multiple_of(k * tn, tn)
        s = jnp.dot(qa, yat_ref[:, pl.ds(j, tn)], preferred_element_type=jnp.float32)
        z = s + ra + ca_ref[:, pl.ds(j, tn)] + jnp.maximum(cb_ref[:, pl.ds(j, tn)] - rb, 0.0)
        m_new = jnp.maximum(m, jnp.max(z, axis=1, keepdims=True))
        l = l * jnp.exp(m - m_new) + jnp.sum(jnp.exp(z - m_new), axis=1, keepdims=True)
        return m_new, l

    m0 = jnp.full((tm, 1), -jnp.inf, jnp.float32)
    l0 = jnp.zeros((tm, 1), jnp.float32)
    m, l = lax.fori_loop(0, n // tn, body, (m0, l0))
    out_ref[...] = m + jnp.log(l)


def row_lse(qa, yat, rb, cb, ra, ca, tm=128, tn=512):
    nr, kq = qa.shape
    n = yat.shape[1]
    return pl.pallas_call(
        functools.partial(_row_lse_kernel, tn=tn),
        grid=(nr // tm,),
        in_specs=[
            pl.BlockSpec((tm, kq), lambda i: (i, 0)),
            pl.BlockSpec((kq, n), lambda i: (0, 0)),
            pl.BlockSpec((tm, 1), lambda i: (i, 0)),
            pl.BlockSpec((1, n), lambda i: (0, 0)),
            pl.BlockSpec((tm, 1), lambda i: (i, 0)),
            pl.BlockSpec((1, n), lambda i: (0, 0)),
        ],
        out_specs=pl.BlockSpec((tm, 1), lambda i: (i, 0)),
        out_shape=jax.ShapeDtypeStruct((nr, 1), jnp.float32),
        interpret=INTERPRET,
    )(qa, yat, rb[:, None], cb[None, :], ra[:, None], ca[None, :])[:, 0]


def _col_lse_kernel(qa_ref, yat_ref, rb_ref, cb_ref, ra_ref, ca_ref, out_ref, *, tm):
    tn = yat_ref.shape[1]
    nr = qa_ref.shape[0]
    yat = yat_ref[...]
    cb = cb_ref[...]
    ca = ca_ref[...]

    def body(k, carry):
        m, l = carry
        i = pl.multiple_of(k * tm, tm)
        s = jnp.dot(qa_ref[pl.ds(i, tm), :], yat, preferred_element_type=jnp.float32)
        z = s + ra_ref[pl.ds(i, tm), :] + ca + jnp.maximum(cb - rb_ref[pl.ds(i, tm), :], 0.0)
        m_new = jnp.maximum(m, jnp.max(z, axis=0, keepdims=True))
        l = l * jnp.exp(m - m_new) + jnp.sum(jnp.exp(z - m_new), axis=0, keepdims=True)
        return m_new, l

    m0 = jnp.full((1, tn), -jnp.inf, jnp.float32)
    l0 = jnp.zeros((1, tn), jnp.float32)
    m, l = lax.fori_loop(0, nr // tm, body, (m0, l0))
    out_ref[...] = m + jnp.log(l)


def col_lse(qa, yat, rb, cb, ra, ca, tm=128, tn=512):
    nr, kq = qa.shape
    n = yat.shape[1]
    return pl.pallas_call(
        functools.partial(_col_lse_kernel, tm=tm),
        grid=(n // tn,),
        in_specs=[
            pl.BlockSpec((nr, kq), lambda j: (0, 0)),
            pl.BlockSpec((kq, tn), lambda j: (0, j)),
            pl.BlockSpec((nr, 1), lambda j: (0, 0)),
            pl.BlockSpec((1, tn), lambda j: (0, j)),
            pl.BlockSpec((nr, 1), lambda j: (0, 0)),
            pl.BlockSpec((1, tn), lambda j: (0, j)),
        ],
        out_specs=pl.BlockSpec((1, tn), lambda j: (0, j)),
        out_shape=jax.ShapeDtypeStruct((1, n), jnp.float32),
        interpret=INTERPRET,
    )(qa, yat, rb[:, None], cb[None, :], ra[:, None], ca[None, :])[0]


def _moment_kernel(qa_ref, yat_ref, rb_ref, cb_ref, ra_ref, ca_ref, f_ref, out_ref, *, tn):
    tm = qa_ref.shape[0]
    n = yat_ref.shape[1]
    qa = qa_ref[...]
    rb = rb_ref[...]
    ra = ra_ref[...]

    def body(k, acc):
        j = pl.multiple_of(k * tn, tn)
        s = jnp.dot(qa, yat_ref[:, pl.ds(j, tn)], preferred_element_type=jnp.float32)
        z = s + ra + ca_ref[:, pl.ds(j, tn)] + jnp.maximum(cb_ref[:, pl.ds(j, tn)] - rb, 0.0)
        plan = jnp.exp(z).astype(jnp.bfloat16)
        return acc + jnp.dot(plan, f_ref[pl.ds(j, tn), :], preferred_element_type=jnp.float32)

    acc = lax.fori_loop(0, n // tn, body, jnp.zeros((tm, f_ref.shape[1]), jnp.float32))
    out_ref[...] = acc


def moments(qa, yat, rb, cb, ra, ca, feats, tm=128, tn=512):
    nr, kq = qa.shape
    n = yat.shape[1]
    nf = feats.shape[1]
    return pl.pallas_call(
        functools.partial(_moment_kernel, tn=tn),
        grid=(nr // tm,),
        in_specs=[
            pl.BlockSpec((tm, kq), lambda i: (i, 0)),
            pl.BlockSpec((kq, n), lambda i: (0, 0)),
            pl.BlockSpec((tm, 1), lambda i: (i, 0)),
            pl.BlockSpec((1, n), lambda i: (0, 0)),
            pl.BlockSpec((tm, 1), lambda i: (i, 0)),
            pl.BlockSpec((1, n), lambda i: (0, 0)),
            pl.BlockSpec((n, nf), lambda i: (0, 0)),
        ],
        out_specs=pl.BlockSpec((tm, nf), lambda i: (i, 0)),
        out_shape=jax.ShapeDtypeStruct((nr, nf), jnp.float32),
        interpret=INTERPRET,
    )(qa, yat, rb[:, None], cb[None, :], ra[:, None], ca[None, :], feats)


def merge_lse(parts):
    top = jnp.max(parts, axis=0)
    return top + jnp.log(jnp.sum(jnp.exp(parts - top[None, :]), axis=0))


def on_device(x_points, y_points, row_mass, col_mass, multipliers, col_potential, basket, damping):
    width = x_points.shape[1]
    share = x_points.shape[0]
    x_pack = jnp.concatenate([x_points, multipliers, row_mass[:, None]], axis=1)
    x_rows_pack = gather_col(x_pack)
    x_rows = x_rows_pack[:, :width]
    mult_rows = x_rows_pack[:, width : 2 * width]
    mass_rows = x_rows_pack[:, 2 * width]
    ny = y_points.shape[0]
    own_rmass = jnp.zeros((ny,), jnp.bfloat16).at[:share].set(row_mass)
    y_pack = jnp.concatenate(
        [y_points, col_potential[:, None], col_mass[:, None], own_rmass[:, None]], axis=1
    )
    y_cols_pack = gather_row(y_pack)
    y_cols = y_cols_pack[:, :width]
    pot_cols = y_cols_pack[:, width].astype(jnp.float32)
    mass_cols = y_cols_pack[:, width + 1].astype(jnp.float32)
    rmass_part = jnp.sum(y_cols_pack[:, width + 2].astype(jnp.float32))

    xf = x_rows.astype(jnp.float32)
    hf = mult_rows.astype(jnp.float32)
    yf = y_cols.astype(jnp.float32)
    row_term2 = 2.0 * (-jnp.sum(hf * xf, axis=1) - KAPPA / width * jnp.sum(xf * xf, axis=1))
    row_basket2 = 2.0 * jnp.sum(xf * basket[None, :], axis=1)
    col_term2 = 2.0 * (-(KAPPA / width) * jnp.sum(yf * yf, axis=1))
    col_basket2 = 2.0 * jnp.sum(yf * basket[None, :], axis=1)
    q_core = jnp.concatenate([mult_rows * 2, x_rows * (2.0 * KAPPA / width * 2.0)], axis=1)
    y_t = y_cols.T
    y_core_t = jnp.concatenate([y_t, y_t], axis=0)
    ny_cols = y_cols.shape[0]
    features = jnp.concatenate(
        [yf, yf * yf, jnp.ones((ny_cols, 1), jnp.float32),
         jnp.zeros((ny_cols, KF - 2 * width - 1), jnp.float32)], axis=1
    ).astype(jnp.bfloat16)

    row_weight = mass_rows.astype(jnp.float32)
    log_row = jnp.log(row_weight)
    log_col = jnp.log(mass_cols)
    nrows = x_rows.shape[0]

    gshift = col_term2 + pot_cols / EPS + log_col
    row_local = row_lse(q_core, y_core_t, row_basket2, col_basket2, row_term2, gshift)
    nu_part = jnp.sum(mass_cols)
    row_msg = jnp.concatenate([row_local, jnp.stack([nu_part, rmass_part])])
    row_all = gather_col(row_msg[None, :])
    nu_total = jnp.sum(row_all[:, nrows])
    mu_total = jnp.sum(row_all[:, nrows + 1])
    log_nu_total = jnp.log(nu_total)
    row_potential = -EPS * (merge_lse(row_all[:, :nrows]) - log_nu_total)
    fshift = row_term2 + row_potential / EPS + log_row

    col_local = col_lse(q_core, y_core_t, row_basket2, col_basket2, fshift, col_term2)
    col_all = gather_row(col_local[None, :])
    col_potential_new = -EPS * (merge_lse(col_all) - jnp.log(mu_total))
    gq = col_term2 + col_potential_new / EPS + log_col - log_nu_total
    fq = row_term2 + row_potential / EPS

    both = moments(q_core, y_core_t, row_basket2, col_basket2, fq, gq, features)
    both = both[:, : 2 * width + 1]
    own = lax.psum_scatter(both, COL, scatter_dimension=0, tiled=True)
    first = own[:, :width]
    second = own[:, width : 2 * width]
    own_mass = own[:, 2 * width]
    xo = x_points.astype(jnp.float32)
    grad = first - xo * own_mass[:, None]
    curv = (second - 2.0 * xo * first + xo * xo * own_mass[:, None]) / EPS + RIDGE
    multipliers_new = multipliers.astype(jnp.float32) - damping[None, :] * grad / curv
    return (row_potential, col_potential_new, multipliers_new)


def solution(mesh):
    nrow, ncol = mesh.devices.shape
    split = Mesh(mesh.devices.reshape(nrow // 4, 4, ncol // 2, 2), ROW + COL)
    placed = (
        P(ROW + COL, None),
        P(COL + ROW, None),
        P(ROW + COL),
        P(COL + ROW),
        P(ROW + COL, None),
        P(COL + ROW),
        P(),
        P(),
    )
    return jax.shard_map(
        on_device,
        mesh=split,
        in_specs=placed,
        out_specs=(P(ROW), P(COL), P(ROW + COL, None)),
        check_vma=False,
    )
```

```python
import functools

import jax
import jax.numpy as jnp
from jax import lax
from jax.experimental import pallas as pl
from jax.sharding import Mesh, PartitionSpec as P

EPS = 0.5
KAPPA = 0.5
RIDGE = 1.0


ROW = ("z", "x")
COL = ("y", "core")


def gather_row(value):
    inner = lax.all_gather(value, ROW[1], axis=0, tiled=True)
    return lax.all_gather(inner, ROW[0], axis=0, tiled=True)


def gather_row_z_first(value):
    inner = lax.all_gather(value, ROW[0], axis=0)
    outer = lax.all_gather(inner, ROW[1], axis=0)
    outer = jnp.swapaxes(outer, 0, 1)
    return outer.reshape((-1,) + value.shape[1:])


def gather_col(value):
    return lax.all_gather(value, COL, axis=0, tiled=True)


KF = 256
INTERPRET = False


def _row_lse_kernel(qa_ref, yat_ref, rb_ref, cb_ref, ra_ref, ca_ref, out_ref, *, tn):
    tm = qa_ref.shape[0]
    n = yat_ref.shape[1]
    qa = qa_ref[...]
    rb = rb_ref[...]
    ra = ra_ref[...]

    def body(k, carry):
        m, l = carry
        j = pl.multiple_of(k * tn, tn)
        s = jnp.dot(qa, yat_ref[:, pl.ds(j, tn)], preferred_element_type=jnp.float32)
        z = s + ra + ca_ref[:, pl.ds(j, tn)] + jnp.maximum(cb_ref[:, pl.ds(j, tn)] - rb, 0.0)
        m_new = jnp.maximum(m, jnp.max(z, axis=1, keepdims=True))
        l = l * jnp.exp(m - m_new) + jnp.sum(jnp.exp(z - m_new), axis=1, keepdims=True)
        return m_new, l

    m0 = jnp.full((tm, 1), -jnp.inf, jnp.float32)
    l0 = jnp.zeros((tm, 1), jnp.float32)
    m, l = lax.fori_loop(0, n // tn, body, (m0, l0))
    out_ref[...] = m + jnp.log(l)


def row_lse(qa, yat, rb, cb, ra, ca, tm=128, tn=512):
    nr, kq = qa.shape
    n = yat.shape[1]
    return pl.pallas_call(
        functools.partial(_row_lse_kernel, tn=tn),
        grid=(nr // tm,),
        in_specs=[
            pl.BlockSpec((tm, kq), lambda i: (i, 0)),
            pl.BlockSpec((kq, n), lambda i: (0, 0)),
            pl.BlockSpec((tm, 1), lambda i: (i, 0)),
            pl.BlockSpec((1, n), lambda i: (0, 0)),
            pl.BlockSpec((tm, 1), lambda i: (i, 0)),
            pl.BlockSpec((1, n), lambda i: (0, 0)),
        ],
        out_specs=pl.BlockSpec((tm, 1), lambda i: (i, 0)),
        out_shape=jax.ShapeDtypeStruct((nr, 1), jnp.float32),
        interpret=INTERPRET,
    )(qa, yat, rb[:, None], cb[None, :], ra[:, None], ca[None, :])[:, 0]


def _col_lse_kernel(qa_ref, yat_ref, rb_ref, cb_ref, ra_ref, ca_ref, out_ref, *, tm):
    tn = yat_ref.shape[1]
    nr = qa_ref.shape[0]
    yat = yat_ref[...]
    cb = cb_ref[...]
    ca = ca_ref[...]

    def body(k, carry):
        m, l = carry
        i = pl.multiple_of(k * tm, tm)
        s = jnp.dot(qa_ref[pl.ds(i, tm), :], yat, preferred_element_type=jnp.float32)
        z = s + ra_ref[pl.ds(i, tm), :] + ca + jnp.maximum(cb - rb_ref[pl.ds(i, tm), :], 0.0)
        m_new = jnp.maximum(m, jnp.max(z, axis=0, keepdims=True))
        l = l * jnp.exp(m - m_new) + jnp.sum(jnp.exp(z - m_new), axis=0, keepdims=True)
        return m_new, l

    m0 = jnp.full((1, tn), -jnp.inf, jnp.float32)
    l0 = jnp.zeros((1, tn), jnp.float32)
    m, l = lax.fori_loop(0, nr // tm, body, (m0, l0))
    out_ref[...] = m + jnp.log(l)


def col_lse(qa, yat, rb, cb, ra, ca, tm=128, tn=512):
    nr, kq = qa.shape
    n = yat.shape[1]
    tn = min(tn, n)
    return pl.pallas_call(
        functools.partial(_col_lse_kernel, tm=tm),
        grid=(n // tn,),
        in_specs=[
            pl.BlockSpec((nr, kq), lambda j: (0, 0)),
            pl.BlockSpec((kq, tn), lambda j: (0, j)),
            pl.BlockSpec((nr, 1), lambda j: (0, 0)),
            pl.BlockSpec((1, tn), lambda j: (0, j)),
            pl.BlockSpec((nr, 1), lambda j: (0, 0)),
            pl.BlockSpec((1, tn), lambda j: (0, j)),
        ],
        out_specs=pl.BlockSpec((1, tn), lambda j: (0, j)),
        out_shape=jax.ShapeDtypeStruct((1, n), jnp.float32),
        interpret=INTERPRET,
    )(qa, yat, rb[:, None], cb[None, :], ra[:, None], ca[None, :])[0]


def _moment_kernel(qa_ref, yat_ref, rb_ref, cb_ref, ra_ref, ca_ref, f_ref, out_ref, *, tn):
    tm = qa_ref.shape[0]
    n = yat_ref.shape[1]
    qa = qa_ref[...]
    rb = rb_ref[...]
    ra = ra_ref[...]

    def body(k, acc):
        j = pl.multiple_of(k * tn, tn)
        s = jnp.dot(qa, yat_ref[:, pl.ds(j, tn)], preferred_element_type=jnp.float32)
        z = s + ra + ca_ref[:, pl.ds(j, tn)] + jnp.maximum(cb_ref[:, pl.ds(j, tn)] - rb, 0.0)
        plan = jnp.exp(z).astype(jnp.bfloat16)
        return acc + jnp.dot(plan, f_ref[pl.ds(j, tn), :], preferred_element_type=jnp.float32)

    acc = lax.fori_loop(0, n // tn, body, jnp.zeros((tm, f_ref.shape[1]), jnp.float32))
    out_ref[...] = acc


def moments(qa, yat, rb, cb, ra, ca, feats, tm=128, tn=512):
    nr, kq = qa.shape
    n = yat.shape[1]
    nf = feats.shape[1]
    return pl.pallas_call(
        functools.partial(_moment_kernel, tn=tn),
        grid=(nr // tm,),
        in_specs=[
            pl.BlockSpec((tm, kq), lambda i: (i, 0)),
            pl.BlockSpec((kq, n), lambda i: (0, 0)),
            pl.BlockSpec((tm, 1), lambda i: (i, 0)),
            pl.BlockSpec((1, n), lambda i: (0, 0)),
            pl.BlockSpec((tm, 1), lambda i: (i, 0)),
            pl.BlockSpec((1, n), lambda i: (0, 0)),
            pl.BlockSpec((n, nf), lambda i: (0, 0)),
        ],
        out_specs=pl.BlockSpec((tm, nf), lambda i: (i, 0)),
        out_shape=jax.ShapeDtypeStruct((nr, nf), jnp.float32),
        interpret=INTERPRET,
    )(qa, yat, rb[:, None], cb[None, :], ra[:, None], ca[None, :], feats)


def merge_lse(parts):
    top = jnp.max(parts, axis=0)
    return top + jnp.log(jnp.sum(jnp.exp(parts - top[None, :]), axis=0))


def on_device(x_points, y_points, row_mass, col_mass, multipliers, col_potential, basket, damping):
    width = x_points.shape[1]
    share = x_points.shape[0]
    x_pack = jnp.concatenate([x_points, multipliers, row_mass[:, None]], axis=1)
    x_rows_pack = gather_col(x_pack)
    x_rows = x_rows_pack[:, :width]
    mult_rows = x_rows_pack[:, width : 2 * width]
    mass_rows = x_rows_pack[:, 2 * width]
    ny = y_points.shape[0]
    own_rmass = jnp.zeros((ny,), jnp.bfloat16).at[:share].set(row_mass)
    y_pack = jnp.concatenate(
        [y_points, col_potential[:, None], col_mass[:, None], own_rmass[:, None]], axis=1
    )
    y_cols_pack = gather_row_z_first(y_pack)
    y_cols = y_cols_pack[:, :width]
    pot_cols = y_cols_pack[:, width].astype(jnp.float32)
    mass_cols = y_cols_pack[:, width + 1].astype(jnp.float32)
    rmass_part = jnp.sum(y_cols_pack[:, width + 2].astype(jnp.float32))

    xf = x_rows.astype(jnp.float32)
    hf = mult_rows.astype(jnp.float32)
    yf = y_cols.astype(jnp.float32)
    row_term2 = 2.0 * (-jnp.sum(hf * xf, axis=1) - KAPPA / width * jnp.sum(xf * xf, axis=1))
    row_basket2 = 2.0 * jnp.sum(xf * basket[None, :], axis=1)
    col_term2 = 2.0 * (-(KAPPA / width) * jnp.sum(yf * yf, axis=1))
    col_basket2 = 2.0 * jnp.sum(yf * basket[None, :], axis=1)
    q_core = jnp.concatenate([mult_rows * 2, x_rows * (2.0 * KAPPA / width * 2.0)], axis=1)
    y_t = y_cols.T
    y_core_t = jnp.concatenate([y_t, y_t], axis=0)
    ny_cols = y_cols.shape[0]
    features = jnp.concatenate(
        [yf, yf * yf, jnp.ones((ny_cols, 1), jnp.float32),
         jnp.zeros((ny_cols, KF - 2 * width - 1), jnp.float32)], axis=1
    ).astype(jnp.bfloat16)

    row_weight = mass_rows.astype(jnp.float32)
    log_row = jnp.log(row_weight)
    log_col = jnp.log(mass_cols)
    nrows = x_rows.shape[0]

    gshift = col_term2 + pot_cols / EPS + log_col
    y_core = jnp.concatenate([y_cols, y_cols], axis=1)
    row_local = col_lse(y_core, q_core.T, -col_basket2, -row_basket2, gshift, row_term2)
    nu_part = jnp.sum(mass_cols)
    row_msg = jnp.concatenate([row_local, jnp.stack([nu_part, rmass_part])])
    row_all = gather_col(row_msg[None, :])
    nu_total = jnp.sum(row_all[:, nrows])
    mu_total = jnp.sum(row_all[:, nrows + 1])
    log_nu_total = jnp.log(nu_total)
    row_potential = -EPS * (merge_lse(row_all[:, :nrows]) - log_nu_total)
    fshift = row_term2 + row_potential / EPS + log_row

    col_local = col_lse(q_core, y_core_t, row_basket2, col_basket2, fshift, col_term2)
    col_all = gather_row(col_local[None, :])
    col_potential_new = -EPS * (merge_lse(col_all) - jnp.log(mu_total))
    gq = col_term2 + col_potential_new / EPS + log_col - log_nu_total
    fq = row_term2 + row_potential / EPS

    both = moments(q_core, y_core_t, row_basket2, col_basket2, fq, gq, features)
    both = both[:, : 2 * width + 1]
    own = lax.psum_scatter(both, COL, scatter_dimension=0, tiled=True)
    first = own[:, :width]
    second = own[:, width : 2 * width]
    own_mass = own[:, 2 * width]
    xo = x_points.astype(jnp.float32)
    grad = first - xo * own_mass[:, None]
    curv = (second - 2.0 * xo * first + xo * xo * own_mass[:, None]) / EPS + RIDGE
    multipliers_new = multipliers.astype(jnp.float32) - damping[None, :] * grad / curv
    return (row_potential, col_potential_new, multipliers_new)


def solution(mesh):
    nrow, ncol = mesh.devices.shape
    split = Mesh(mesh.devices.reshape(nrow // 4, 4, ncol // 2, 2), ROW + COL)
    placed = (
        P(ROW + COL, None),
        P(COL + ROW, None),
        P(ROW + COL),
        P(COL + ROW),
        P(ROW + COL, None),
        P(COL + ROW),
        P(),
        P(),
    )
    return jax.shard_map(
        on_device,
        mesh=split,
        in_specs=placed,
        out_specs=(P(ROW), P(COL), P(ROW + COL, None)),
        check_vma=False,
    )
```

```python
import functools

import jax
import jax.numpy as jnp
from jax import lax
from jax.experimental import pallas as pl
from jax.sharding import Mesh, PartitionSpec as P

EPS = 0.5
KAPPA = 0.5
RIDGE = 1.0


ROW = ("z", "x")
COL = ("y", "core")


def gather_row(value):
    inner = lax.all_gather(value, ROW[1], axis=0, tiled=True)
    return lax.all_gather(inner, ROW[0], axis=0, tiled=True)


def gather_row_z_first(value):
    inner = lax.all_gather(value, ROW[0], axis=0)
    outer = lax.all_gather(inner, ROW[1], axis=0)
    outer = jnp.swapaxes(outer, 0, 1)
    return outer.reshape((-1,) + value.shape[1:])


def gather_col(value):
    return lax.all_gather(value, COL, axis=0, tiled=True)


KF = 256
INTERPRET = False


def _row_lse_kernel(qa_ref, yat_ref, rb_ref, cb_ref, ra_ref, ca_ref, out_ref, *, tn):
    tm = qa_ref.shape[0]
    n = yat_ref.shape[1]
    qa = qa_ref[...]
    rb = rb_ref[...]
    ra = ra_ref[...]

    def body(k, carry):
        m, l = carry
        j = pl.multiple_of(k * tn, tn)
        s = jnp.dot(qa, yat_ref[:, pl.ds(j, tn)], preferred_element_type=jnp.float32)
        z = s + ra + ca_ref[:, pl.ds(j, tn)] + jnp.maximum(cb_ref[:, pl.ds(j, tn)] - rb, 0.0)
        m_new = jnp.maximum(m, jnp.max(z, axis=1, keepdims=True))
        l = l * jnp.exp(m - m_new) + jnp.sum(jnp.exp(z - m_new), axis=1, keepdims=True)
        return m_new, l

    m0 = jnp.full((tm, 1), -jnp.inf, jnp.float32)
    l0 = jnp.zeros((tm, 1), jnp.float32)
    m, l = lax.fori_loop(0, n // tn, body, (m0, l0))
    out_ref[...] = m + jnp.log(l)


def row_lse(qa, yat, rb, cb, ra, ca, tm=128, tn=512):
    nr, kq = qa.shape
    n = yat.shape[1]
    return pl.pallas_call(
        functools.partial(_row_lse_kernel, tn=tn),
        grid=(nr // tm,),
        in_specs=[
            pl.BlockSpec((tm, kq), lambda i: (i, 0)),
            pl.BlockSpec((kq, n), lambda i: (0, 0)),
            pl.BlockSpec((tm, 1), lambda i: (i, 0)),
            pl.BlockSpec((1, n), lambda i: (0, 0)),
            pl.BlockSpec((tm, 1), lambda i: (i, 0)),
            pl.BlockSpec((1, n), lambda i: (0, 0)),
        ],
        out_specs=pl.BlockSpec((tm, 1), lambda i: (i, 0)),
        out_shape=jax.ShapeDtypeStruct((nr, 1), jnp.float32),
        interpret=INTERPRET,
    )(qa, yat, rb[:, None], cb[None, :], ra[:, None], ca[None, :])[:, 0]


def _col_lse_kernel(qa_ref, yat_ref, rb_ref, cb_ref, ra_ref, ca_ref, out_ref, *, tm):
    tn = yat_ref.shape[1]
    nr = qa_ref.shape[0]
    yat = yat_ref[...]
    cb = cb_ref[...]
    ca = ca_ref[...]

    def body(k, carry):
        m, l = carry
        i = pl.multiple_of(k * tm, tm)
        s = jnp.dot(qa_ref[pl.ds(i, tm), :], yat, preferred_element_type=jnp.float32)
        z = s + ra_ref[pl.ds(i, tm), :] + ca + jnp.maximum(cb - rb_ref[pl.ds(i, tm), :], 0.0)
        m_new = jnp.maximum(m, jnp.max(z, axis=0, keepdims=True))
        l = l * jnp.exp(m - m_new) + jnp.sum(jnp.exp(z - m_new), axis=0, keepdims=True)
        return m_new, l

    m0 = jnp.full((1, tn), -jnp.inf, jnp.float32)
    l0 = jnp.zeros((1, tn), jnp.float32)
    m, l = lax.fori_loop(0, nr // tm, body, (m0, l0))
    out_ref[...] = m + jnp.log(l)


def col_lse(qa, yat, rb, cb, ra, ca, tm=512, tn=1024):
    nr, kq = qa.shape
    n = yat.shape[1]
    tm = min(tm, nr)
    tn = min(tn, n)
    return pl.pallas_call(
        functools.partial(_col_lse_kernel, tm=tm),
        grid=(n // tn,),
        in_specs=[
            pl.BlockSpec((nr, kq), lambda j: (0, 0)),
            pl.BlockSpec((kq, tn), lambda j: (0, j)),
            pl.BlockSpec((nr, 1), lambda j: (0, 0)),
            pl.BlockSpec((1, tn), lambda j: (0, j)),
            pl.BlockSpec((nr, 1), lambda j: (0, 0)),
            pl.BlockSpec((1, tn), lambda j: (0, j)),
        ],
        out_specs=pl.BlockSpec((1, tn), lambda j: (0, j)),
        out_shape=jax.ShapeDtypeStruct((1, n), jnp.float32),
        interpret=INTERPRET,
    )(qa, yat, rb[:, None], cb[None, :], ra[:, None], ca[None, :])[0]


def _moment_kernel(qa_ref, yat_ref, rb_ref, cb_ref, ra_ref, ca_ref, f_ref, out_ref, *, tn):
    tm = qa_ref.shape[0]
    n = yat_ref.shape[1]
    qa = qa_ref[...]
    rb = rb_ref[...]
    ra = ra_ref[...]

    def body(k, acc):
        j = pl.multiple_of(k * tn, tn)
        s = jnp.dot(qa, yat_ref[:, pl.ds(j, tn)], preferred_element_type=jnp.float32)
        z = s + ra + ca_ref[:, pl.ds(j, tn)] + jnp.maximum(cb_ref[:, pl.ds(j, tn)] - rb, 0.0)
        plan = jnp.exp(z).astype(jnp.bfloat16)
        return acc + jnp.dot(plan, f_ref[pl.ds(j, tn), :], preferred_element_type=jnp.float32)

    acc = lax.fori_loop(0, n // tn, body, jnp.zeros((tm, f_ref.shape[1]), jnp.float32))
    out_ref[...] = acc


def moments(qa, yat, rb, cb, ra, ca, feats, tm=512, tn=2048):
    nr, kq = qa.shape
    n = yat.shape[1]
    tm = min(tm, nr)
    tn = min(tn, n)
    nf = feats.shape[1]
    return pl.pallas_call(
        functools.partial(_moment_kernel, tn=tn),
        grid=(nr // tm,),
        in_specs=[
            pl.BlockSpec((tm, kq), lambda i: (i, 0)),
            pl.BlockSpec((kq, n), lambda i: (0, 0)),
            pl.BlockSpec((tm, 1), lambda i: (i, 0)),
            pl.BlockSpec((1, n), lambda i: (0, 0)),
            pl.BlockSpec((tm, 1), lambda i: (i, 0)),
            pl.BlockSpec((1, n), lambda i: (0, 0)),
            pl.BlockSpec((n, nf), lambda i: (0, 0)),
        ],
        out_specs=pl.BlockSpec((tm, nf), lambda i: (i, 0)),
        out_shape=jax.ShapeDtypeStruct((nr, nf), jnp.float32),
        interpret=INTERPRET,
    )(qa, yat, rb[:, None], cb[None, :], ra[:, None], ca[None, :], feats)


def merge_lse(parts):
    top = jnp.max(parts, axis=0)
    return top + jnp.log(jnp.sum(jnp.exp(parts - top[None, :]), axis=0))


def on_device(x_points, y_points, row_mass, col_mass, multipliers, col_potential, basket, damping):
    width = x_points.shape[1]
    share = x_points.shape[0]
    x_pack = jnp.concatenate([x_points, multipliers, row_mass[:, None]], axis=1)
    x_rows_pack = gather_col(x_pack)
    x_rows = x_rows_pack[:, :width]
    mult_rows = x_rows_pack[:, width : 2 * width]
    mass_rows = x_rows_pack[:, 2 * width]
    ny = y_points.shape[0]
    own_rmass = jnp.zeros((ny,), jnp.bfloat16).at[:share].set(row_mass)
    y_pack = jnp.concatenate(
        [y_points, col_potential[:, None], col_mass[:, None], own_rmass[:, None]], axis=1
    )
    y_cols_pack = gather_row_z_first(y_pack)
    y_cols = y_cols_pack[:, :width]
    pot_cols = y_cols_pack[:, width].astype(jnp.float32)
    mass_cols = y_cols_pack[:, width + 1].astype(jnp.float32)
    rmass_part = jnp.sum(y_cols_pack[:, width + 2].astype(jnp.float32))

    xf = x_rows.astype(jnp.float32)
    hf = mult_rows.astype(jnp.float32)
    yf = y_cols.astype(jnp.float32)
    row_term2 = 2.0 * (-jnp.sum(hf * xf, axis=1) - KAPPA / width * jnp.sum(xf * xf, axis=1))
    row_basket2 = 2.0 * jnp.sum(xf * basket[None, :], axis=1)
    col_term2 = 2.0 * (-(KAPPA / width) * jnp.sum(yf * yf, axis=1))
    col_basket2 = 2.0 * jnp.sum(yf * basket[None, :], axis=1)
    q_core = jnp.concatenate([mult_rows * 2, x_rows * (2.0 * KAPPA / width * 2.0)], axis=1)
    y_t = y_cols.T
    y_core_t = jnp.concatenate([y_t, y_t], axis=0)
    ny_cols = y_cols.shape[0]
    features = jnp.concatenate(
        [yf, yf * yf, jnp.ones((ny_cols, 1), jnp.float32),
         jnp.zeros((ny_cols, KF - 2 * width - 1), jnp.float32)], axis=1
    ).astype(jnp.bfloat16)

    row_weight = mass_rows.astype(jnp.float32)
    log_row = jnp.log(row_weight)
    log_col = jnp.log(mass_cols)
    nrows = x_rows.shape[0]

    gshift = col_term2 + pot_cols / EPS + log_col
    y_core = jnp.concatenate([y_cols, y_cols], axis=1)
    row_local = col_lse(y_core, q_core.T, -col_basket2, -row_basket2, gshift, row_term2)
    nu_part = jnp.sum(mass_cols)
    row_msg = jnp.concatenate([row_local, jnp.stack([nu_part, rmass_part])])
    row_all = gather_col(row_msg[None, :])
    nu_total = jnp.sum(row_all[:, nrows])
    mu_total = jnp.sum(row_all[:, nrows + 1])
    log_nu_total = jnp.log(nu_total)
    row_potential = -EPS * (merge_lse(row_all[:, :nrows]) - log_nu_total)
    fshift = row_term2 + row_potential / EPS + log_row

    col_local = col_lse(q_core, y_core_t, row_basket2, col_basket2, fshift, col_term2)
    col_all = gather_row(col_local[None, :])
    col_potential_new = -EPS * (merge_lse(col_all) - jnp.log(mu_total))
    gq = col_term2 + col_potential_new / EPS + log_col - log_nu_total
    fq = row_term2 + row_potential / EPS

    both = moments(q_core, y_core_t, row_basket2, col_basket2, fq, gq, features)
    both = both[:, : 2 * width + 1]
    own = lax.psum_scatter(both, COL, scatter_dimension=0, tiled=True)
    first = own[:, :width]
    second = own[:, width : 2 * width]
    own_mass = own[:, 2 * width]
    xo = x_points.astype(jnp.float32)
    grad = first - xo * own_mass[:, None]
    curv = (second - 2.0 * xo * first + xo * xo * own_mass[:, None]) / EPS + RIDGE
    multipliers_new = multipliers.astype(jnp.float32) - damping[None, :] * grad / curv
    return (row_potential, col_potential_new, multipliers_new)


def solution(mesh):
    nrow, ncol = mesh.devices.shape
    split = Mesh(mesh.devices.reshape(nrow // 4, 4, ncol // 2, 2), ROW + COL)
    placed = (
        P(ROW + COL, None),
        P(COL + ROW, None),
        P(ROW + COL),
        P(COL + ROW),
        P(ROW + COL, None),
        P(COL + ROW),
        P(),
        P(),
    )
    return jax.shard_map(
        on_device,
        mesh=split,
        in_specs=placed,
        out_specs=(P(ROW), P(COL), P(ROW + COL, None)),
        check_vma=False,
    )
```

```python
import functools

import jax
import jax.numpy as jnp
from jax import lax
from jax.experimental import pallas as pl
from jax.sharding import Mesh, PartitionSpec as P

EPS = 0.5
KAPPA = 0.5
RIDGE = 1.0


ROW = ("z", "x")
COL = ("y", "core")


def gather_row(value):
    inner = lax.all_gather(value, ROW[1], axis=0, tiled=True)
    return lax.all_gather(inner, ROW[0], axis=0, tiled=True)


def gather_col(value):
    return lax.all_gather(value, COL, axis=0, tiled=True)


KF = 256
INTERPRET = False


def _row_lse_kernel(qa_ref, yat_ref, rb_ref, cb_ref, ra_ref, ca_ref, out_ref, *, tn):
    tm = qa_ref.shape[0]
    n = yat_ref.shape[1]
    qa = qa_ref[...]
    rb = rb_ref[...]
    ra = ra_ref[...]

    def body(k, carry):
        m, l = carry
        j = pl.multiple_of(k * tn, tn)
        s = jnp.dot(qa, yat_ref[:, pl.ds(j, tn)], preferred_element_type=jnp.float32)
        z = s + ra + ca_ref[:, pl.ds(j, tn)] + jnp.maximum(cb_ref[:, pl.ds(j, tn)] - rb, 0.0)
        m_new = jnp.maximum(m, jnp.max(z, axis=1, keepdims=True))
        l = l * jnp.exp(m - m_new) + jnp.sum(jnp.exp(z - m_new), axis=1, keepdims=True)
        return m_new, l

    m0 = jnp.full((tm, 1), -jnp.inf, jnp.float32)
    l0 = jnp.zeros((tm, 1), jnp.float32)
    m, l = lax.fori_loop(0, n // tn, body, (m0, l0))
    out_ref[...] = m + jnp.log(l)


def row_lse(qa, yat, rb, cb, ra, ca, tm=512, tn=2048):
    nr, kq = qa.shape
    n = yat.shape[1]
    tm = min(tm, nr)
    tn = min(tn, n)
    return pl.pallas_call(
        functools.partial(_row_lse_kernel, tn=tn),
        grid=(nr // tm,),
        in_specs=[
            pl.BlockSpec((tm, kq), lambda i: (i, 0)),
            pl.BlockSpec((kq, n), lambda i: (0, 0)),
            pl.BlockSpec((tm, 1), lambda i: (i, 0)),
            pl.BlockSpec((1, n), lambda i: (0, 0)),
            pl.BlockSpec((tm, 1), lambda i: (i, 0)),
            pl.BlockSpec((1, n), lambda i: (0, 0)),
        ],
        out_specs=pl.BlockSpec((tm, 1), lambda i: (i, 0)),
        out_shape=jax.ShapeDtypeStruct((nr, 1), jnp.float32),
        interpret=INTERPRET,
    )(qa, yat, rb[:, None], cb[None, :], ra[:, None], ca[None, :])[:, 0]


def _col_lse_kernel(qa_ref, yat_ref, rb_ref, cb_ref, ra_ref, ca_ref, out_ref, *, tm):
    tn = yat_ref.shape[1]
    nr = qa_ref.shape[0]
    yat = yat_ref[...]
    cb = cb_ref[...]
    ca = ca_ref[...]

    def body(k, carry):
        m, l = carry
        i = pl.multiple_of(k * tm, tm)
        s = jnp.dot(qa_ref[pl.ds(i, tm), :], yat, preferred_element_type=jnp.float32)
        z = s + ra_ref[pl.ds(i, tm), :] + ca + jnp.maximum(cb - rb_ref[pl.ds(i, tm), :], 0.0)
        m_new = jnp.maximum(m, jnp.max(z, axis=0, keepdims=True))
        l = l * jnp.exp(m - m_new) + jnp.sum(jnp.exp(z - m_new), axis=0, keepdims=True)
        return m_new, l

    m0 = jnp.full((1, tn), -jnp.inf, jnp.float32)
    l0 = jnp.zeros((1, tn), jnp.float32)
    m, l = lax.fori_loop(0, nr // tm, body, (m0, l0))
    out_ref[...] = m + jnp.log(l)


def col_lse(qa, yat, rb, cb, ra, ca, tm=512, tn=1024):
    nr, kq = qa.shape
    n = yat.shape[1]
    tm = min(tm, nr)
    tn = min(tn, n)
    return pl.pallas_call(
        functools.partial(_col_lse_kernel, tm=tm),
        grid=(n // tn,),
        in_specs=[
            pl.BlockSpec((nr, kq), lambda j: (0, 0)),
            pl.BlockSpec((kq, tn), lambda j: (0, j)),
            pl.BlockSpec((nr, 1), lambda j: (0, 0)),
            pl.BlockSpec((1, tn), lambda j: (0, j)),
            pl.BlockSpec((nr, 1), lambda j: (0, 0)),
            pl.BlockSpec((1, tn), lambda j: (0, j)),
        ],
        out_specs=pl.BlockSpec((1, tn), lambda j: (0, j)),
        out_shape=jax.ShapeDtypeStruct((1, n), jnp.float32),
        interpret=INTERPRET,
    )(qa, yat, rb[:, None], cb[None, :], ra[:, None], ca[None, :])[0]


def _moment_kernel(qa_ref, yat_ref, rb_ref, cb_ref, ra_ref, ca_ref, f_ref, out_ref, *, tn):
    tm = qa_ref.shape[0]
    n = yat_ref.shape[1]
    qa = qa_ref[...]
    rb = rb_ref[...]
    ra = ra_ref[...]

    def body(k, acc):
        j = pl.multiple_of(k * tn, tn)
        s = jnp.dot(qa, yat_ref[:, pl.ds(j, tn)], preferred_element_type=jnp.float32)
        z = s + ra + ca_ref[:, pl.ds(j, tn)] + jnp.maximum(cb_ref[:, pl.ds(j, tn)] - rb, 0.0)
        plan = jnp.exp(z).astype(jnp.bfloat16)
        return acc + jnp.dot(plan, f_ref[pl.ds(j, tn), :], preferred_element_type=jnp.float32)

    acc = lax.fori_loop(0, n // tn, body, jnp.zeros((tm, f_ref.shape[1]), jnp.float32))
    out_ref[...] = acc


def moments(qa, yat, rb, cb, ra, ca, feats, tm=512, tn=2048):
    nr, kq = qa.shape
    n = yat.shape[1]
    tm = min(tm, nr)
    tn = min(tn, n)
    nf = feats.shape[1]
    return pl.pallas_call(
        functools.partial(_moment_kernel, tn=tn),
        grid=(nr // tm,),
        in_specs=[
            pl.BlockSpec((tm, kq), lambda i: (i, 0)),
            pl.BlockSpec((kq, n), lambda i: (0, 0)),
            pl.BlockSpec((tm, 1), lambda i: (i, 0)),
            pl.BlockSpec((1, n), lambda i: (0, 0)),
            pl.BlockSpec((tm, 1), lambda i: (i, 0)),
            pl.BlockSpec((1, n), lambda i: (0, 0)),
            pl.BlockSpec((n, nf), lambda i: (0, 0)),
        ],
        out_specs=pl.BlockSpec((tm, nf), lambda i: (i, 0)),
        out_shape=jax.ShapeDtypeStruct((nr, nf), jnp.float32),
        interpret=INTERPRET,
    )(qa, yat, rb[:, None], cb[None, :], ra[:, None], ca[None, :], feats)


def merge_lse(parts):
    top = jnp.max(parts, axis=0)
    return top + jnp.log(jnp.sum(jnp.exp(parts - top[None, :]), axis=0))


def on_device(x_points, y_points, row_mass, col_mass, multipliers, col_potential, basket, damping):
    width = x_points.shape[1]
    share = x_points.shape[0]
    x_pack = jnp.concatenate([x_points, multipliers, row_mass[:, None]], axis=1)
    x_rows_pack = gather_col(x_pack)
    x_rows = x_rows_pack[:, :width]
    mult_rows = x_rows_pack[:, width : 2 * width]
    mass_rows = x_rows_pack[:, 2 * width]
    ny = y_points.shape[0]
    own_rmass = jnp.zeros((ny,), jnp.bfloat16).at[:share].set(row_mass)
    y_pack = jnp.concatenate(
        [y_points, col_potential[:, None], col_mass[:, None], own_rmass[:, None]], axis=1
    )
    y_cols_pack = gather_row(y_pack)
    y_cols = y_cols_pack[:, :width]
    pot_cols = y_cols_pack[:, width].astype(jnp.float32)
    mass_cols = y_cols_pack[:, width + 1].astype(jnp.float32)
    rmass_part = jnp.sum(y_cols_pack[:, width + 2].astype(jnp.float32))

    xf = x_rows.astype(jnp.float32)
    hf = mult_rows.astype(jnp.float32)
    yf = y_cols.astype(jnp.float32)
    row_term2 = 2.0 * (-jnp.sum(hf * xf, axis=1) - KAPPA / width * jnp.sum(xf * xf, axis=1))
    row_basket2 = 2.0 * jnp.sum(xf * basket[None, :], axis=1)
    col_term2 = 2.0 * (-(KAPPA / width) * jnp.sum(yf * yf, axis=1))
    col_basket2 = 2.0 * jnp.sum(yf * basket[None, :], axis=1)
    q_core = jnp.concatenate([mult_rows * 2, x_rows * (2.0 * KAPPA / width * 2.0)], axis=1)
    y_t = y_cols.T
    y_core_t = jnp.concatenate([y_t, y_t], axis=0)
    ny_cols = y_cols.shape[0]
    features = jnp.concatenate(
        [yf, yf * yf, jnp.ones((ny_cols, 1), jnp.float32),
         jnp.zeros((ny_cols, KF - 2 * width - 1), jnp.float32)], axis=1
    ).astype(jnp.bfloat16)

    row_weight = mass_rows.astype(jnp.float32)
    log_row = jnp.log(row_weight)
    log_col = jnp.log(mass_cols)
    nrows = x_rows.shape[0]

    gshift = col_term2 + pot_cols / EPS + log_col
    row_local = row_lse(q_core, y_core_t, row_basket2, col_basket2, row_term2, gshift)
    nu_part = jnp.sum(mass_cols)
    row_msg = jnp.concatenate([row_local, jnp.stack([nu_part, rmass_part])])
    row_all = gather_col(row_msg[None, :])
    nu_total = jnp.sum(row_all[:, nrows])
    mu_total = jnp.sum(row_all[:, nrows + 1])
    log_nu_total = jnp.log(nu_total)
    row_potential = -EPS * (merge_lse(row_all[:, :nrows]) - log_nu_total)
    fshift = row_term2 + row_potential / EPS + log_row

    col_local = col_lse(q_core, y_core_t, row_basket2, col_basket2, fshift, col_term2)
    col_all = gather_row(col_local[None, :])
    col_potential_new = -EPS * (merge_lse(col_all) - jnp.log(mu_total))
    gq = col_term2 + col_potential_new / EPS + log_col - log_nu_total
    fq = row_term2 + row_potential / EPS

    both = moments(q_core, y_core_t, row_basket2, col_basket2, fq, gq, features)
    both = both[:, : 2 * width + 1]
    own = lax.psum_scatter(both, COL, scatter_dimension=0, tiled=True)
    first = own[:, :width]
    second = own[:, width : 2 * width]
    own_mass = own[:, 2 * width]
    xo = x_points.astype(jnp.float32)
    grad = first - xo * own_mass[:, None]
    curv = (second - 2.0 * xo * first + xo * xo * own_mass[:, None]) / EPS + RIDGE
    multipliers_new = multipliers.astype(jnp.float32) - damping[None, :] * grad / curv
    return (row_potential, col_potential_new, multipliers_new)


def solution(mesh):
    nrow, ncol = mesh.devices.shape
    split = Mesh(mesh.devices.reshape(nrow // 4, 4, ncol // 2, 2), ROW + COL)
    placed = (
        P(ROW + COL, None),
        P(COL + ROW, None),
        P(ROW + COL),
        P(COL + ROW),
        P(ROW + COL, None),
        P(COL + ROW),
        P(),
        P(),
    )
    return jax.shard_map(
        on_device,
        mesh=split,
        in_specs=placed,
        out_specs=(P(ROW), P(COL), P(ROW + COL, None)),
        check_vma=False,
    )
```

```python
import functools

import jax
import jax.numpy as jnp
from jax import lax
from jax.experimental import pallas as pl
from jax.sharding import Mesh, PartitionSpec as P


EPS = 0.5
KAPPA = 0.5
RIDGE = 1.0


ROW = ("z", "x")
COL = ("y", "core")


def gather_row(value):
    inner = lax.all_gather(value, ROW[1], axis=0, tiled=True)
    return lax.all_gather(inner, ROW[0], axis=0, tiled=True)


def gather_col(value):
    inner = lax.all_gather(value, COL[1], axis=0, tiled=True)
    return lax.all_gather(inner, COL[0], axis=0, tiled=True)


KF = 256
INTERPRET = False


def _row_lse_kernel(qa_ref, yat_ref, rb_ref, cb_ref, ra_ref, ca_ref, out_ref, *, tn):
    tm = qa_ref.shape[0]
    n = yat_ref.shape[1]
    qa = qa_ref[...]
    rb = rb_ref[...]
    ra = ra_ref[...]

    def body(k, carry):
        m, l = carry
        j = pl.multiple_of(k * tn, tn)
        s = jnp.dot(qa, yat_ref[:, pl.ds(j, tn)], preferred_element_type=jnp.float32)
        z = s + ra + ca_ref[:, pl.ds(j, tn)] + jnp.maximum(cb_ref[:, pl.ds(j, tn)] - rb, 0.0)
        m_new = jnp.maximum(m, jnp.max(z, axis=1, keepdims=True))
        l = l * jnp.exp(m - m_new) + jnp.sum(jnp.exp(z - m_new), axis=1, keepdims=True)
        return m_new, l

    m0 = jnp.full((tm, 1), -jnp.inf, jnp.float32)
    l0 = jnp.zeros((tm, 1), jnp.float32)
    m, l = lax.fori_loop(0, n // tn, body, (m0, l0))
    out_ref[...] = m + jnp.log(l)


def row_lse(qa, yat, rb, cb, ra, ca, tm=512, tn=2048):
    nr, kq = qa.shape
    n = yat.shape[1]
    tm = min(tm, nr)
    tn = min(tn, n)
    return pl.pallas_call(
        functools.partial(_row_lse_kernel, tn=tn),
        grid=(nr // tm,),
        in_specs=[
            pl.BlockSpec((tm, kq), lambda i: (i, 0)),
            pl.BlockSpec((kq, n), lambda i: (0, 0)),
            pl.BlockSpec((tm, 1), lambda i: (i, 0)),
            pl.BlockSpec((1, n), lambda i: (0, 0)),
            pl.BlockSpec((tm, 1), lambda i: (i, 0)),
            pl.BlockSpec((1, n), lambda i: (0, 0)),
        ],
        out_specs=pl.BlockSpec((tm, 1), lambda i: (i, 0)),
        out_shape=jax.ShapeDtypeStruct((nr, 1), jnp.float32),
        interpret=INTERPRET,
    )(qa, yat, rb[:, None], cb[None, :], ra[:, None], ca[None, :])[:, 0]


def _col_lse_kernel(qa_ref, yat_ref, rb_ref, cb_ref, ra_ref, ca_ref, out_ref, *, tm):
    tn = yat_ref.shape[1]
    nr = qa_ref.shape[0]
    yat = yat_ref[...]
    cb = cb_ref[...]
    ca = ca_ref[...]

    def body(k, carry):
        m, l = carry
        i = pl.multiple_of(k * tm, tm)
        s = jnp.dot(qa_ref[pl.ds(i, tm), :], yat, preferred_element_type=jnp.float32)
        z = s + ra_ref[pl.ds(i, tm), :] + ca + jnp.maximum(cb - rb_ref[pl.ds(i, tm), :], 0.0)
        m_new = jnp.maximum(m, jnp.max(z, axis=0, keepdims=True))
        l = l * jnp.exp(m - m_new) + jnp.sum(jnp.exp(z - m_new), axis=0, keepdims=True)
        return m_new, l

    m0 = jnp.full((1, tn), -jnp.inf, jnp.float32)
    l0 = jnp.zeros((1, tn), jnp.float32)
    m, l = lax.fori_loop(0, nr // tm, body, (m0, l0))
    out_ref[...] = m + jnp.log(l)


def col_lse(qa, yat, rb, cb, ra, ca, tm=512, tn=1024):
    nr, kq = qa.shape
    n = yat.shape[1]
    tm = min(tm, nr)
    tn = min(tn, n)
    return pl.pallas_call(
        functools.partial(_col_lse_kernel, tm=tm),
        grid=(n // tn,),
        in_specs=[
            pl.BlockSpec((nr, kq), lambda j: (0, 0)),
            pl.BlockSpec((kq, tn), lambda j: (0, j)),
            pl.BlockSpec((nr, 1), lambda j: (0, 0)),
            pl.BlockSpec((1, tn), lambda j: (0, j)),
            pl.BlockSpec((nr, 1), lambda j: (0, 0)),
            pl.BlockSpec((1, tn), lambda j: (0, j)),
        ],
        out_specs=pl.BlockSpec((1, tn), lambda j: (0, j)),
        out_shape=jax.ShapeDtypeStruct((1, n), jnp.float32),
        interpret=INTERPRET,
    )(qa, yat, rb[:, None], cb[None, :], ra[:, None], ca[None, :])[0]


def _moment_kernel(qa_ref, yat_ref, rb_ref, cb_ref, ra_ref, ca_ref, f_ref, out_ref, *, tn):
    tm = qa_ref.shape[0]
    n = yat_ref.shape[1]
    qa = qa_ref[...]
    rb = rb_ref[...]
    ra = ra_ref[...]

    def body(k, acc):
        j = pl.multiple_of(k * tn, tn)
        s = jnp.dot(qa, yat_ref[:, pl.ds(j, tn)], preferred_element_type=jnp.float32)
        z = s + ra + ca_ref[:, pl.ds(j, tn)] + jnp.maximum(cb_ref[:, pl.ds(j, tn)] - rb, 0.0)
        plan = jnp.exp(z).astype(jnp.bfloat16)
        return acc + jnp.dot(plan, f_ref[pl.ds(j, tn), :], preferred_element_type=jnp.float32)

    acc = lax.fori_loop(0, n // tn, body, jnp.zeros((tm, f_ref.shape[1]), jnp.float32))
    out_ref[...] = acc


def moments(qa, yat, rb, cb, ra, ca, feats, tm=512, tn=2048):
    nr, kq = qa.shape
    n = yat.shape[1]
    tm = min(tm, nr)
    tn = min(tn, n)
    nf = feats.shape[1]
    return pl.pallas_call(
        functools.partial(_moment_kernel, tn=tn),
        grid=(nr // tm,),
        in_specs=[
            pl.BlockSpec((tm, kq), lambda i: (i, 0)),
            pl.BlockSpec((kq, n), lambda i: (0, 0)),
            pl.BlockSpec((tm, 1), lambda i: (i, 0)),
            pl.BlockSpec((1, n), lambda i: (0, 0)),
            pl.BlockSpec((tm, 1), lambda i: (i, 0)),
            pl.BlockSpec((1, n), lambda i: (0, 0)),
            pl.BlockSpec((n, nf), lambda i: (0, 0)),
        ],
        out_specs=pl.BlockSpec((tm, nf), lambda i: (i, 0)),
        out_shape=jax.ShapeDtypeStruct((nr, nf), jnp.float32),
        interpret=INTERPRET,
    )(qa, yat, rb[:, None], cb[None, :], ra[:, None], ca[None, :], feats)


def merge_lse(parts):
    top = jnp.max(parts, axis=0)
    return top + jnp.log(jnp.sum(jnp.exp(parts - top[None, :]), axis=0))


def sweep(x_points, y_points, row_mass, col_mass, multipliers, col_potential, basket, damping):
    width = x_points.shape[1]
    share = x_points.shape[0]
    x_pack = jnp.concatenate([x_points, multipliers, row_mass[:, None]], axis=1)
    x_rows_pack = lax.all_gather(x_pack, COL, axis=0, tiled=True)
    x_rows = x_rows_pack[:, :width]
    mult_rows = x_rows_pack[:, width : 2 * width]
    mass_rows = x_rows_pack[:, 2 * width]
    ny = y_points.shape[0]
    own_rmass = jnp.zeros((ny,), jnp.bfloat16).at[:share].set(row_mass)
    y_pack = jnp.concatenate(
        [y_points, col_potential[:, None], col_mass[:, None], own_rmass[:, None]], axis=1
    )
    y_cols_pack = gather_row(y_pack)
    y_cols = y_cols_pack[:, :width]
    pot_cols = y_cols_pack[:, width].astype(jnp.float32)
    mass_cols = y_cols_pack[:, width + 1].astype(jnp.float32)
    rmass_part = jnp.sum(y_cols_pack[:, width + 2].astype(jnp.float32))

    xf = x_rows.astype(jnp.float32)
    hf = mult_rows.astype(jnp.float32)
    yf = y_cols.astype(jnp.float32)
    row_term2 = 2.0 * (-jnp.sum(hf * xf, axis=1) - KAPPA / width * jnp.sum(xf * xf, axis=1))
    row_basket2 = 2.0 * jnp.sum(xf * basket[None, :], axis=1)
    col_term2 = 2.0 * (-(KAPPA / width) * jnp.sum(yf * yf, axis=1))
    col_basket2 = 2.0 * jnp.sum(yf * basket[None, :], axis=1)
    q_core = jnp.concatenate([mult_rows * 2, x_rows * (2.0 * KAPPA / width * 2.0)], axis=1)
    y_t = y_cols.T
    y_core_t = jnp.concatenate([y_t, y_t], axis=0)
    ny_cols = y_cols.shape[0]
    features = jnp.concatenate(
        [yf, yf * yf, jnp.ones((ny_cols, 1), jnp.float32),
         jnp.zeros((ny_cols, KF - 2 * width - 1), jnp.float32)], axis=1
    ).astype(jnp.bfloat16)

    row_weight = mass_rows.astype(jnp.float32)
    log_row = jnp.log(row_weight)
    log_col = jnp.log(mass_cols)
    nrows = x_rows.shape[0]

    gshift = col_term2 + pot_cols / EPS + log_col
    row_local = row_lse(q_core, y_core_t, row_basket2, col_basket2, row_term2, gshift)
    nu_part = jnp.sum(mass_cols)
    row_msg = jnp.concatenate([row_local, jnp.stack([nu_part, rmass_part])])
    row_all = gather_col(row_msg[None, :])
    nu_total = jnp.sum(row_all[:, nrows])
    mu_total = jnp.sum(row_all[:, nrows + 1])
    log_nu_total = jnp.log(nu_total)
    row_potential = -EPS * (merge_lse(row_all[:, :nrows]) - log_nu_total)
    fshift = row_term2 + row_potential / EPS + log_row

    col_local = col_lse(q_core, y_core_t, row_basket2, col_basket2, fshift, col_term2)
    col_all = gather_row(col_local[None, :])
    col_potential_new = -EPS * (merge_lse(col_all) - jnp.log(mu_total))
    gq = col_term2 + col_potential_new / EPS + log_col - log_nu_total
    fq = row_term2 + row_potential / EPS

    both = moments(q_core, y_core_t, row_basket2, col_basket2, fq, gq, features)
    both = both[:, : 2 * width + 1]
    own = lax.psum_scatter(both, COL, scatter_dimension=0, tiled=True)
    first = own[:, :width]
    second = own[:, width : 2 * width]
    own_mass = own[:, 2 * width]
    xo = x_points.astype(jnp.float32)
    grad = first - xo * own_mass[:, None]
    curv = (second - 2.0 * xo * first + xo * xo * own_mass[:, None]) / EPS + RIDGE
    multipliers_new = multipliers.astype(jnp.float32) - damping[None, :] * grad / curv
    return (row_potential, col_potential_new, multipliers_new)


def solution(mesh):
    nrow, ncol = mesh.devices.shape
    split = Mesh(mesh.devices.reshape(nrow // 4, 4, ncol // 2, 2), ROW + COL)
    placed = (
        P(ROW + COL, None),
        P(COL + ROW, None),
        P(ROW + COL),
        P(COL + ROW),
        P(ROW + COL, None),
        P(COL + ROW),
        P(),
        P(),
    )
    return jax.shard_map(
        sweep,
        mesh=split,
        in_specs=placed,
        out_specs=(P(ROW), P(COL), P(ROW + COL, None)),
        check_vma=False,
    )
```

```python
import functools

import jax
import jax.numpy as jnp
from jax import lax
from jax.experimental import pallas as pl
from jax.sharding import Mesh, PartitionSpec as P


EPS = 0.5
KAPPA = 0.5
RIDGE = 1.0


ROW = ("z", "x")
COL = ("y", "core")


def gather_row(value):
    inner = lax.all_gather(value, ROW[1], axis=0, tiled=True)
    return lax.all_gather(inner, ROW[0], axis=0, tiled=True)


KF = 256
INTERPRET = False


def _row_lse_kernel(qa_ref, yat_ref, rb_ref, cb_ref, ra_ref, ca_ref, out_ref, *, tn):
    tm = qa_ref.shape[0]
    n = yat_ref.shape[1]
    qa = qa_ref[...]
    rb = rb_ref[...]
    ra = ra_ref[...]

    def body(k, carry):
        m, l = carry
        j = pl.multiple_of(k * tn, tn)
        s = jnp.dot(qa, yat_ref[:, pl.ds(j, tn)], preferred_element_type=jnp.float32)
        z = s + ra + ca_ref[:, pl.ds(j, tn)] + jnp.maximum(cb_ref[:, pl.ds(j, tn)] - rb, 0.0)
        m_new = jnp.maximum(m, jnp.max(z, axis=1, keepdims=True))
        l = l * jnp.exp(m - m_new) + jnp.sum(jnp.exp(z - m_new), axis=1, keepdims=True)
        return m_new, l

    m0 = jnp.full((tm, 1), -jnp.inf, jnp.float32)
    l0 = jnp.zeros((tm, 1), jnp.float32)
    m, l = lax.fori_loop(0, n // tn, body, (m0, l0))
    out_ref[...] = m + jnp.log(l)


def row_lse(qa, yat, rb, cb, ra, ca, tm=512, tn=2048):
    nr, kq = qa.shape
    n = yat.shape[1]
    tm = min(tm, nr)
    tn = min(tn, n)
    return pl.pallas_call(
        functools.partial(_row_lse_kernel, tn=tn),
        grid=(nr // tm,),
        in_specs=[
            pl.BlockSpec((tm, kq), lambda i: (i, 0)),
            pl.BlockSpec((kq, n), lambda i: (0, 0)),
            pl.BlockSpec((tm, 1), lambda i: (i, 0)),
            pl.BlockSpec((1, n), lambda i: (0, 0)),
            pl.BlockSpec((tm, 1), lambda i: (i, 0)),
            pl.BlockSpec((1, n), lambda i: (0, 0)),
        ],
        out_specs=pl.BlockSpec((tm, 1), lambda i: (i, 0)),
        out_shape=jax.ShapeDtypeStruct((nr, 1), jnp.float32),
        interpret=INTERPRET,
    )(qa, yat, rb[:, None], cb[None, :], ra[:, None], ca[None, :])[:, 0]


def _col_lse_kernel(qa_ref, yat_ref, rb_ref, cb_ref, ra_ref, ca_ref, out_ref, *, tm):
    tn = yat_ref.shape[1]
    nr = qa_ref.shape[0]
    yat = yat_ref[...]
    cb = cb_ref[...]
    ca = ca_ref[...]

    def body(k, carry):
        m, l = carry
        i = pl.multiple_of(k * tm, tm)
        s = jnp.dot(qa_ref[pl.ds(i, tm), :], yat, preferred_element_type=jnp.float32)
        z = s + ra_ref[pl.ds(i, tm), :] + ca + jnp.maximum(cb - rb_ref[pl.ds(i, tm), :], 0.0)
        m_new = jnp.maximum(m, jnp.max(z, axis=0, keepdims=True))
        l = l * jnp.exp(m - m_new) + jnp.sum(jnp.exp(z - m_new), axis=0, keepdims=True)
        return m_new, l

    m0 = jnp.full((1, tn), -jnp.inf, jnp.float32)
    l0 = jnp.zeros((1, tn), jnp.float32)
    m, l = lax.fori_loop(0, nr // tm, body, (m0, l0))
    out_ref[...] = m + jnp.log(l)


def col_lse(qa, yat, rb, cb, ra, ca, tm=512, tn=1024):
    nr, kq = qa.shape
    n = yat.shape[1]
    tm = min(tm, nr)
    tn = min(tn, n)
    return pl.pallas_call(
        functools.partial(_col_lse_kernel, tm=tm),
        grid=(n // tn,),
        in_specs=[
            pl.BlockSpec((nr, kq), lambda j: (0, 0)),
            pl.BlockSpec((kq, tn), lambda j: (0, j)),
            pl.BlockSpec((nr, 1), lambda j: (0, 0)),
            pl.BlockSpec((1, tn), lambda j: (0, j)),
            pl.BlockSpec((nr, 1), lambda j: (0, 0)),
            pl.BlockSpec((1, tn), lambda j: (0, j)),
        ],
        out_specs=pl.BlockSpec((1, tn), lambda j: (0, j)),
        out_shape=jax.ShapeDtypeStruct((1, n), jnp.float32),
        interpret=INTERPRET,
    )(qa, yat, rb[:, None], cb[None, :], ra[:, None], ca[None, :])[0]


def _moment_kernel(qa_ref, yat_ref, rb_ref, cb_ref, ra_ref, ca_ref, f_ref, out_ref, *, tn):
    tm = qa_ref.shape[0]
    n = yat_ref.shape[1]
    qa = qa_ref[...]
    rb = rb_ref[...]
    ra = ra_ref[...]

    def body(k, acc):
        j = pl.multiple_of(k * tn, tn)
        s = jnp.dot(qa, yat_ref[:, pl.ds(j, tn)], preferred_element_type=jnp.float32)
        z = s + ra + ca_ref[:, pl.ds(j, tn)] + jnp.maximum(cb_ref[:, pl.ds(j, tn)] - rb, 0.0)
        plan = jnp.exp(z).astype(jnp.bfloat16)
        return acc + jnp.dot(plan, f_ref[pl.ds(j, tn), :], preferred_element_type=jnp.float32)

    acc = lax.fori_loop(0, n // tn, body, jnp.zeros((tm, f_ref.shape[1]), jnp.float32))
    out_ref[...] = acc


def moments(qa, yat, rb, cb, ra, ca, feats, tm=512, tn=2048):
    nr, kq = qa.shape
    n = yat.shape[1]
    tm = min(tm, nr)
    tn = min(tn, n)
    nf = feats.shape[1]
    return pl.pallas_call(
        functools.partial(_moment_kernel, tn=tn),
        grid=(nr // tm,),
        in_specs=[
            pl.BlockSpec((tm, kq), lambda i: (i, 0)),
            pl.BlockSpec((kq, n), lambda i: (0, 0)),
            pl.BlockSpec((tm, 1), lambda i: (i, 0)),
            pl.BlockSpec((1, n), lambda i: (0, 0)),
            pl.BlockSpec((tm, 1), lambda i: (i, 0)),
            pl.BlockSpec((1, n), lambda i: (0, 0)),
            pl.BlockSpec((n, nf), lambda i: (0, 0)),
        ],
        out_specs=pl.BlockSpec((tm, nf), lambda i: (i, 0)),
        out_shape=jax.ShapeDtypeStruct((nr, nf), jnp.float32),
        interpret=INTERPRET,
    )(qa, yat, rb[:, None], cb[None, :], ra[:, None], ca[None, :], feats)


def merge_lse(parts):
    top = jnp.max(parts, axis=0)
    return top + jnp.log(jnp.sum(jnp.exp(parts - top[None, :]), axis=0))


def sweep(x_points, y_points, row_mass, col_mass, multipliers, col_potential, basket, damping):
    width = x_points.shape[1]
    share = x_points.shape[0]
    x_pack = jnp.concatenate([x_points, multipliers, row_mass[:, None]], axis=1)
    x_rows_pack = lax.all_gather(x_pack, COL, axis=0, tiled=True)
    x_rows = x_rows_pack[:, :width]
    mult_rows = x_rows_pack[:, width : 2 * width]
    mass_rows = x_rows_pack[:, 2 * width]
    ny = y_points.shape[0]
    own_rmass = jnp.zeros((ny,), jnp.bfloat16).at[:share].set(row_mass)
    y_pack = jnp.concatenate(
        [y_points, col_potential[:, None], col_mass[:, None], own_rmass[:, None]], axis=1
    )
    y_cols_pack = gather_row(y_pack)
    y_cols = y_cols_pack[:, :width]
    pot_cols = y_cols_pack[:, width].astype(jnp.float32)
    mass_cols = y_cols_pack[:, width + 1].astype(jnp.float32)
    rmass_part = jnp.sum(y_cols_pack[:, width + 2].astype(jnp.float32))

    xf = x_rows.astype(jnp.float32)
    hf = mult_rows.astype(jnp.float32)
    row_term2 = 2.0 * (-jnp.sum(hf * xf, axis=1) - KAPPA / width * jnp.sum(xf * xf, axis=1))
    row_basket2 = 2.0 * jnp.sum(xf * basket[None, :], axis=1)
    q_core = jnp.concatenate([mult_rows * 2, x_rows * (2.0 * KAPPA / width * 2.0)], axis=1)
    log_row = jnp.log(mass_rows.astype(jnp.float32))
    yf = y_cols.astype(jnp.float32)
    col_term2 = 2.0 * (-(KAPPA / width) * jnp.sum(yf * yf, axis=1))
    col_basket2 = 2.0 * jnp.sum(yf * basket[None, :], axis=1)
    y_t = y_cols.T
    y_core_t = jnp.concatenate([y_t, y_t], axis=0)
    ny_cols = y_cols.shape[0]
    features = jnp.concatenate(
        [yf, yf * yf, jnp.ones((ny_cols, 1), jnp.float32),
         jnp.zeros((ny_cols, KF - 2 * width - 1), jnp.float32)], axis=1
    ).astype(jnp.bfloat16)

    log_col = jnp.log(mass_cols)
    nrows = x_rows.shape[0]

    gshift = col_term2 + pot_cols / EPS + log_col
    row_local = row_lse(q_core, y_core_t, row_basket2, col_basket2, row_term2, gshift)
    nu_part = jnp.sum(mass_cols)
    row_msg = jnp.concatenate([row_local, jnp.stack([nu_part, rmass_part])])
    row_core = lax.all_gather(row_msg, COL[1], axis=0)
    row_msg = jnp.concatenate([merge_lse(row_core[:, :nrows]), jnp.sum(row_core[:, nrows:], axis=0)])
    row_all = lax.all_gather(row_msg, COL[0], axis=0)
    nu_total = jnp.sum(row_all[:, nrows])
    mu_total = jnp.sum(row_all[:, nrows + 1])
    log_nu_total = jnp.log(nu_total)
    row_potential = -EPS * (merge_lse(row_all[:, :nrows]) - log_nu_total)
    fshift = row_term2 + row_potential / EPS + log_row

    col_local = col_lse(q_core, y_core_t, row_basket2, col_basket2, fshift, col_term2)
    col_x = merge_lse(lax.all_gather(col_local, ROW[1], axis=0))
    col_all = lax.all_gather(col_x, ROW[0], axis=0)
    col_potential_new = -EPS * (merge_lse(col_all) - jnp.log(mu_total))
    gq = col_term2 + col_potential_new / EPS + log_col - log_nu_total
    fq = row_term2 + row_potential / EPS

    both = moments(q_core, y_core_t, row_basket2, col_basket2, fq, gq, features)
    both = both[:, : 2 * width + 1]
    own = lax.psum_scatter(both, COL, scatter_dimension=0, tiled=True)
    first = own[:, :width]
    second = own[:, width : 2 * width]
    own_mass = own[:, 2 * width]
    xo = x_points.astype(jnp.float32)
    grad = first - xo * own_mass[:, None]
    curv = (second - 2.0 * xo * first + xo * xo * own_mass[:, None]) / EPS + RIDGE
    multipliers_new = multipliers.astype(jnp.float32) - damping[None, :] * grad / curv
    return (row_potential, col_potential_new, multipliers_new)


def solution(mesh):
    nrow, ncol = mesh.devices.shape
    split = Mesh(mesh.devices.reshape(nrow // 4, 4, ncol // 2, 2), ROW + COL)
    placed = (
        P(ROW + COL, None),
        P(COL + ROW, None),
        P(ROW + COL),
        P(COL + ROW),
        P(ROW + COL, None),
        P(COL + ROW),
        P(),
        P(),
    )
    return jax.shard_map(
        sweep,
        mesh=split,
        in_specs=placed,
        out_specs=(P(ROW), P(COL), P(ROW + COL, None)),
        check_vma=False,
    )
```

```python
import functools

import jax
import jax.numpy as jnp
from jax import lax
from jax.experimental import pallas as pl
from jax.sharding import Mesh, PartitionSpec as P


EPS = 0.5
KAPPA = 0.5
RIDGE = 1.0


ROW = ("z", "x")
COL = ("y", "core")


def gather_row(value):
    inner = lax.all_gather(value, ROW[1], axis=0, tiled=True)
    return lax.all_gather(inner, ROW[0], axis=0, tiled=True)


def gather_col(value):
    inner = lax.all_gather(value, COL[1], axis=0, tiled=True)
    return lax.all_gather(inner, COL[0], axis=0, tiled=True)


KF = 256
INTERPRET = False


def _row_lse_kernel(qa_ref, yat_ref, rb_ref, cb_ref, ra_ref, ca_ref, out_ref, *, tn):
    tm = qa_ref.shape[0]
    n = yat_ref.shape[1]
    qa = qa_ref[...]
    rb = rb_ref[...]
    ra = ra_ref[...]

    def body(k, carry):
        m, l = carry
        j = pl.multiple_of(k * tn, tn)
        s = jnp.dot(qa, yat_ref[:, pl.ds(j, tn)], preferred_element_type=jnp.float32)
        z = s + ra + ca_ref[:, pl.ds(j, tn)] + jnp.maximum(cb_ref[:, pl.ds(j, tn)] - rb, 0.0)
        m_new = jnp.maximum(m, jnp.max(z, axis=1, keepdims=True))
        l = l * jnp.exp(m - m_new) + jnp.sum(jnp.exp(z - m_new), axis=1, keepdims=True)
        return m_new, l

    m0 = jnp.full((tm, 1), -jnp.inf, jnp.float32)
    l0 = jnp.zeros((tm, 1), jnp.float32)
    m, l = lax.fori_loop(0, n // tn, body, (m0, l0))
    out_ref[...] = m + jnp.log(l)


def row_lse(qa, yat, rb, cb, ra, ca, tm=512, tn=2048):
    nr, kq = qa.shape
    n = yat.shape[1]
    tm = min(tm, nr)
    tn = min(tn, n)
    return pl.pallas_call(
        functools.partial(_row_lse_kernel, tn=tn),
        grid=(nr // tm,),
        in_specs=[
            pl.BlockSpec((tm, kq), lambda i: (i, 0)),
            pl.BlockSpec((kq, n), lambda i: (0, 0)),
            pl.BlockSpec((tm, 1), lambda i: (i, 0)),
            pl.BlockSpec((1, n), lambda i: (0, 0)),
            pl.BlockSpec((tm, 1), lambda i: (i, 0)),
            pl.BlockSpec((1, n), lambda i: (0, 0)),
        ],
        out_specs=pl.BlockSpec((tm, 1), lambda i: (i, 0)),
        out_shape=jax.ShapeDtypeStruct((nr, 1), jnp.float32),
        interpret=INTERPRET,
    )(qa, yat, rb[:, None], cb[None, :], ra[:, None], ca[None, :])[:, 0]


def _col_lse_kernel(qa_ref, yat_ref, rb_ref, cb_ref, ra_ref, ca_ref, out_ref, *, tm):
    tn = yat_ref.shape[1]
    nr = qa_ref.shape[0]
    yat = yat_ref[...]
    cb = cb_ref[...]
    ca = ca_ref[...]

    def body(k, carry):
        m, l = carry
        i = pl.multiple_of(k * tm, tm)
        s = jnp.dot(qa_ref[pl.ds(i, tm), :], yat, preferred_element_type=jnp.float32)
        z = s + ra_ref[pl.ds(i, tm), :] + ca + jnp.maximum(cb - rb_ref[pl.ds(i, tm), :], 0.0)
        m_new = jnp.maximum(m, jnp.max(z, axis=0, keepdims=True))
        l = l * jnp.exp(m - m_new) + jnp.sum(jnp.exp(z - m_new), axis=0, keepdims=True)
        return m_new, l

    m0 = jnp.full((1, tn), -jnp.inf, jnp.float32)
    l0 = jnp.zeros((1, tn), jnp.float32)
    m, l = lax.fori_loop(0, nr // tm, body, (m0, l0))
    out_ref[...] = m + jnp.log(l)


def col_lse(qa, yat, rb, cb, ra, ca, tm=512, tn=1024):
    nr, kq = qa.shape
    n = yat.shape[1]
    tm = min(tm, nr)
    tn = min(tn, n)
    return pl.pallas_call(
        functools.partial(_col_lse_kernel, tm=tm),
        grid=(n // tn,),
        in_specs=[
            pl.BlockSpec((nr, kq), lambda j: (0, 0)),
            pl.BlockSpec((kq, tn), lambda j: (0, j)),
            pl.BlockSpec((nr, 1), lambda j: (0, 0)),
            pl.BlockSpec((1, tn), lambda j: (0, j)),
            pl.BlockSpec((nr, 1), lambda j: (0, 0)),
            pl.BlockSpec((1, tn), lambda j: (0, j)),
        ],
        out_specs=pl.BlockSpec((1, tn), lambda j: (0, j)),
        out_shape=jax.ShapeDtypeStruct((1, n), jnp.float32),
        interpret=INTERPRET,
    )(qa, yat, rb[:, None], cb[None, :], ra[:, None], ca[None, :])[0]


def _moment_kernel(qa_ref, yat_ref, rb_ref, cb_ref, ra_ref, ca_ref, f_ref, out_ref, *, tn):
    tm = qa_ref.shape[0]
    n = yat_ref.shape[1]
    qa = qa_ref[...]
    rb = rb_ref[...]
    ra = ra_ref[...]

    def body(k, acc):
        j = pl.multiple_of(k * tn, tn)
        s = jnp.dot(qa, yat_ref[:, pl.ds(j, tn)], preferred_element_type=jnp.float32)
        z = s + ra + ca_ref[:, pl.ds(j, tn)] + jnp.maximum(cb_ref[:, pl.ds(j, tn)] - rb, 0.0)
        plan = jnp.exp(z).astype(jnp.bfloat16)
        return acc + jnp.dot(plan, f_ref[pl.ds(j, tn), :], preferred_element_type=jnp.float32)

    acc = lax.fori_loop(0, n // tn, body, jnp.zeros((tm, f_ref.shape[1]), jnp.float32))
    out_ref[...] = acc


def moments(qa, yat, rb, cb, ra, ca, feats, tm=512, tn=2048):
    nr, kq = qa.shape
    n = yat.shape[1]
    tm = min(tm, nr)
    tn = min(tn, n)
    nf = feats.shape[1]
    return pl.pallas_call(
        functools.partial(_moment_kernel, tn=tn),
        grid=(nr // tm,),
        in_specs=[
            pl.BlockSpec((tm, kq), lambda i: (i, 0)),
            pl.BlockSpec((kq, n), lambda i: (0, 0)),
            pl.BlockSpec((tm, 1), lambda i: (i, 0)),
            pl.BlockSpec((1, n), lambda i: (0, 0)),
            pl.BlockSpec((tm, 1), lambda i: (i, 0)),
            pl.BlockSpec((1, n), lambda i: (0, 0)),
            pl.BlockSpec((n, nf), lambda i: (0, 0)),
        ],
        out_specs=pl.BlockSpec((tm, nf), lambda i: (i, 0)),
        out_shape=jax.ShapeDtypeStruct((nr, nf), jnp.float32),
        interpret=INTERPRET,
    )(qa, yat, rb[:, None], cb[None, :], ra[:, None], ca[None, :], feats)


def merge_lse(parts):
    top = jnp.max(parts, axis=0)
    return top + jnp.log(jnp.sum(jnp.exp(parts - top[None, :]), axis=0))


def sweep(x_points, y_points, row_mass, col_mass, multipliers, col_potential, basket, damping):
    width = x_points.shape[1]
    share = x_points.shape[0]
    x_pack = jnp.concatenate([x_points, multipliers, row_mass[:, None]], axis=1)
    x_rows_pack = lax.all_gather(x_pack, COL, axis=0, tiled=True)
    x_rows = x_rows_pack[:, :width]
    mult_rows = x_rows_pack[:, width : 2 * width]
    mass_rows = x_rows_pack[:, 2 * width]
    ny = y_points.shape[0]
    own_rmass = jnp.zeros((ny,), jnp.bfloat16).at[:share].set(row_mass)
    y_pack = jnp.concatenate(
        [y_points, col_potential[:, None], col_mass[:, None], own_rmass[:, None]], axis=1
    )
    y_cols_pack = gather_row(y_pack)
    y_cols = y_cols_pack[:, :width]
    pot_cols = y_cols_pack[:, width].astype(jnp.float32)
    mass_cols = y_cols_pack[:, width + 1].astype(jnp.float32)
    rmass_part = jnp.sum(y_cols_pack[:, width + 2].astype(jnp.float32))

    xf = x_rows.astype(jnp.float32)
    hf = mult_rows.astype(jnp.float32)
    row_term2 = 2.0 * (-jnp.sum(hf * xf, axis=1) - KAPPA / width * jnp.sum(xf * xf, axis=1))
    row_basket2 = 2.0 * jnp.sum(xf * basket[None, :], axis=1)
    q_core = jnp.concatenate([mult_rows * 2, x_rows * (2.0 * KAPPA / width * 2.0)], axis=1)
    log_row = jnp.log(mass_rows.astype(jnp.float32))
    yf = y_cols.astype(jnp.float32)
    col_term2 = 2.0 * (-(KAPPA / width) * jnp.sum(yf * yf, axis=1))
    col_basket2 = 2.0 * jnp.sum(yf * basket[None, :], axis=1)
    y_t = y_cols.T
    y_core_t = jnp.concatenate([y_t, y_t], axis=0)
    ny_cols = y_cols.shape[0]
    features = jnp.concatenate(
        [yf, yf * yf, jnp.ones((ny_cols, 1), jnp.float32),
         jnp.zeros((ny_cols, KF - 2 * width - 1), jnp.float32)], axis=1
    ).astype(jnp.bfloat16)

    log_col = jnp.log(mass_cols)
    nrows = x_rows.shape[0]

    gshift = col_term2 + pot_cols / EPS + log_col
    row_local = row_lse(q_core, y_core_t, row_basket2, col_basket2, row_term2, gshift)
    nu_part = jnp.sum(mass_cols)
    row_msg = jnp.concatenate([row_local, jnp.stack([nu_part, rmass_part])])
    row_all = gather_col(row_msg[None, :])
    nu_total = jnp.sum(row_all[:, nrows])
    mu_total = jnp.sum(row_all[:, nrows + 1])
    log_nu_total = jnp.log(nu_total)
    row_potential = -EPS * (merge_lse(row_all[:, :nrows]) - log_nu_total)
    fshift = row_term2 + row_potential / EPS + log_row

    col_local = col_lse(q_core, y_core_t, row_basket2, col_basket2, fshift, col_term2)
    col_x = merge_lse(lax.all_gather(col_local, ROW[1], axis=0))
    col_all = lax.all_gather(col_x, ROW[0], axis=0)
    col_potential_new = -EPS * (merge_lse(col_all) - jnp.log(mu_total))
    gq = col_term2 + col_potential_new / EPS + log_col - log_nu_total
    fq = row_term2 + row_potential / EPS

    both = moments(q_core, y_core_t, row_basket2, col_basket2, fq, gq, features)
    both = both[:, : 2 * width + 1]
    own = lax.psum_scatter(both, COL, scatter_dimension=0, tiled=True)
    first = own[:, :width]
    second = own[:, width : 2 * width]
    own_mass = own[:, 2 * width]
    xo = x_points.astype(jnp.float32)
    grad = first - xo * own_mass[:, None]
    curv = (second - 2.0 * xo * first + xo * xo * own_mass[:, None]) / EPS + RIDGE
    multipliers_new = multipliers.astype(jnp.float32) - damping[None, :] * grad / curv
    return (row_potential, col_potential_new, multipliers_new)


def solution(mesh):
    nrow, ncol = mesh.devices.shape
    split = Mesh(mesh.devices.reshape(nrow // 4, 4, ncol // 2, 2), ROW + COL)
    placed = (
        P(ROW + COL, None),
        P(COL + ROW, None),
        P(ROW + COL),
        P(COL + ROW),
        P(ROW + COL, None),
        P(COL + ROW),
        P(),
        P(),
    )
    return jax.shard_map(
        sweep,
        mesh=split,
        in_specs=placed,
        out_specs=(P(ROW), P(COL), P(ROW + COL, None)),
        check_vma=False,
    )
```

```python
import functools

import jax
import jax.numpy as jnp
from jax import lax
from jax.experimental import pallas as pl
from jax.sharding import Mesh, PartitionSpec as P


EPS = 0.5
KAPPA = 0.5
RIDGE = 1.0


ROW = ("z", "x")
COL = ("y", "core")


def gather_row(value):
    inner = lax.all_gather(value, ROW[1], axis=0, tiled=True)
    return lax.all_gather(inner, ROW[0], axis=0, tiled=True)


def gather_col(value):
    inner = lax.all_gather(value, COL[1], axis=0, tiled=True)
    return lax.all_gather(inner, COL[0], axis=0, tiled=True)


KF = 129
INTERPRET = False


def _row_lse_kernel(qa_ref, yat_ref, rb_ref, cb_ref, ra_ref, ca_ref, out_ref, *, tn):
    tm = qa_ref.shape[0]
    n = yat_ref.shape[0]
    qa = qa_ref[...]
    rb = rb_ref[...]
    ra = ra_ref[...]

    def body(k, carry):
        m, l = carry
        j = pl.multiple_of(k * tn, tn)
        s = lax.dot_general(qa, yat_ref[pl.ds(j, tn), :], (((1,), (1,)), ((), ())), preferred_element_type=jnp.float32)
        z = s + ra + ca_ref[:, pl.ds(j, tn)] + jnp.maximum(cb_ref[:, pl.ds(j, tn)] - rb, 0.0)
        m_new = jnp.maximum(m, jnp.max(z, axis=1, keepdims=True))
        l = l * jnp.exp(m - m_new) + jnp.sum(jnp.exp(z - m_new), axis=1, keepdims=True)
        return m_new, l

    m0 = jnp.full((tm, 1), -jnp.inf, jnp.float32)
    l0 = jnp.zeros((tm, 1), jnp.float32)
    m, l = lax.fori_loop(0, n // tn, body, (m0, l0))
    out_ref[...] = m + jnp.log(l)


def row_lse(qa, yat, rb, cb, ra, ca, tm=512, tn=2048):
    nr, kq = qa.shape
    n = yat.shape[0]
    tm = min(tm, nr)
    tn = min(tn, n)
    return pl.pallas_call(
        functools.partial(_row_lse_kernel, tn=tn),
        grid=(nr // tm,),
        in_specs=[
            pl.BlockSpec((tm, kq), lambda i: (i, 0)),
            pl.BlockSpec((n, kq), lambda i: (0, 0)),
            pl.BlockSpec((tm, 1), lambda i: (i, 0)),
            pl.BlockSpec((1, n), lambda i: (0, 0)),
            pl.BlockSpec((tm, 1), lambda i: (i, 0)),
            pl.BlockSpec((1, n), lambda i: (0, 0)),
        ],
        out_specs=pl.BlockSpec((tm, 1), lambda i: (i, 0)),
        out_shape=jax.ShapeDtypeStruct((nr, 1), jnp.float32),
        interpret=INTERPRET,
    )(qa, yat, rb[:, None], cb[None, :], ra[:, None], ca[None, :])[:, 0]


def _col_lse_kernel(qa_ref, yat_ref, rb_ref, cb_ref, ra_ref, ca_ref, out_ref, *, tm):
    tn = yat_ref.shape[0]
    nr = qa_ref.shape[0]
    yat = yat_ref[...]
    cb = cb_ref[...]
    ca = ca_ref[...]

    def body(k, carry):
        m, l = carry
        i = pl.multiple_of(k * tm, tm)
        s = lax.dot_general(qa_ref[pl.ds(i, tm), :], yat, (((1,), (1,)), ((), ())), preferred_element_type=jnp.float32)
        z = s + ra_ref[pl.ds(i, tm), :] + ca + jnp.maximum(cb - rb_ref[pl.ds(i, tm), :], 0.0)
        m_new = jnp.maximum(m, jnp.max(z, axis=0, keepdims=True))
        l = l * jnp.exp(m - m_new) + jnp.sum(jnp.exp(z - m_new), axis=0, keepdims=True)
        return m_new, l

    m0 = jnp.full((1, tn), -jnp.inf, jnp.float32)
    l0 = jnp.zeros((1, tn), jnp.float32)
    m, l = lax.fori_loop(0, nr // tm, body, (m0, l0))
    out_ref[...] = m + jnp.log(l)


def col_lse(qa, yat, rb, cb, ra, ca, tm=512, tn=1024):
    nr, kq = qa.shape
    n = yat.shape[0]
    tm = min(tm, nr)
    tn = min(tn, n)
    return pl.pallas_call(
        functools.partial(_col_lse_kernel, tm=tm),
        grid=(n // tn,),
        in_specs=[
            pl.BlockSpec((nr, kq), lambda j: (0, 0)),
            pl.BlockSpec((tn, kq), lambda j: (j, 0)),
            pl.BlockSpec((nr, 1), lambda j: (0, 0)),
            pl.BlockSpec((1, tn), lambda j: (0, j)),
            pl.BlockSpec((nr, 1), lambda j: (0, 0)),
            pl.BlockSpec((1, tn), lambda j: (0, j)),
        ],
        out_specs=pl.BlockSpec((1, tn), lambda j: (0, j)),
        out_shape=jax.ShapeDtypeStruct((1, n), jnp.float32),
        interpret=INTERPRET,
    )(qa, yat, rb[:, None], cb[None, :], ra[:, None], ca[None, :])[0]


def _moment_kernel(qa_ref, yat_ref, rb_ref, cb_ref, ra_ref, ca_ref, f_ref, out_ref, *, tn):
    tm = qa_ref.shape[0]
    n = yat_ref.shape[0]
    qa = qa_ref[...]
    rb = rb_ref[...]
    ra = ra_ref[...]

    def body(k, acc):
        j = pl.multiple_of(k * tn, tn)
        s = lax.dot_general(qa, yat_ref[pl.ds(j, tn), :], (((1,), (1,)), ((), ())), preferred_element_type=jnp.float32)
        z = s + ra + ca_ref[:, pl.ds(j, tn)] + jnp.maximum(cb_ref[:, pl.ds(j, tn)] - rb, 0.0)
        plan = jnp.exp(z).astype(jnp.bfloat16)
        return acc + jnp.dot(plan, f_ref[pl.ds(j, tn), :], preferred_element_type=jnp.float32)

    acc = lax.fori_loop(0, n // tn, body, jnp.zeros((tm, f_ref.shape[1]), jnp.float32))
    out_ref[...] = acc


def moments(qa, yat, rb, cb, ra, ca, feats, tm=512, tn=2048):
    nr, kq = qa.shape
    n = yat.shape[0]
    tm = min(tm, nr)
    tn = min(tn, n)
    nf = feats.shape[1]
    return pl.pallas_call(
        functools.partial(_moment_kernel, tn=tn),
        grid=(nr // tm,),
        in_specs=[
            pl.BlockSpec((tm, kq), lambda i: (i, 0)),
            pl.BlockSpec((n, kq), lambda i: (0, 0)),
            pl.BlockSpec((tm, 1), lambda i: (i, 0)),
            pl.BlockSpec((1, n), lambda i: (0, 0)),
            pl.BlockSpec((tm, 1), lambda i: (i, 0)),
            pl.BlockSpec((1, n), lambda i: (0, 0)),
            pl.BlockSpec((n, nf), lambda i: (0, 0)),
        ],
        out_specs=pl.BlockSpec((tm, nf), lambda i: (i, 0)),
        out_shape=jax.ShapeDtypeStruct((nr, nf), jnp.float32),
        interpret=INTERPRET,
    )(qa, yat, rb[:, None], cb[None, :], ra[:, None], ca[None, :], feats)


def merge_lse(parts):
    top = jnp.max(parts, axis=0)
    return top + jnp.log(jnp.sum(jnp.exp(parts - top[None, :]), axis=0))


def sweep(x_points, y_points, row_mass, col_mass, multipliers, col_potential, basket, damping):
    width = x_points.shape[1]
    share = x_points.shape[0]
    x_pack = jnp.concatenate([x_points, multipliers, row_mass[:, None]], axis=1)
    x_rows_pack = lax.all_gather(x_pack, COL, axis=0, tiled=True)
    x_rows = x_rows_pack[:, :width]
    mult_rows = x_rows_pack[:, width : 2 * width]
    mass_rows = x_rows_pack[:, 2 * width]
    ny = y_points.shape[0]
    own_rmass = jnp.zeros((ny,), jnp.bfloat16).at[:share].set(row_mass)
    y_pack = jnp.concatenate(
        [y_points, col_potential[:, None], col_mass[:, None], own_rmass[:, None]], axis=1
    )
    y_cols_pack = gather_row(y_pack)
    y_cols = y_cols_pack[:, :width]
    pot_cols = y_cols_pack[:, width].astype(jnp.float32)
    mass_cols = y_cols_pack[:, width + 1].astype(jnp.float32)
    rmass_part = jnp.sum(y_cols_pack[:, width + 2].astype(jnp.float32))

    xf = x_rows.astype(jnp.float32)
    hf = mult_rows.astype(jnp.float32)
    row_term2 = 2.0 * (-jnp.sum(hf * xf, axis=1) - KAPPA / width * jnp.sum(xf * xf, axis=1))
    row_basket2 = 2.0 * jnp.sum(xf * basket[None, :], axis=1)
    q_core = jnp.concatenate([mult_rows * 2, x_rows * (2.0 * KAPPA / width * 2.0)], axis=1)
    log_row = jnp.log(mass_rows.astype(jnp.float32))
    yf = y_cols.astype(jnp.float32)
    hi = lax.Precision.HIGHEST
    col_term2 = 2.0 * (-(KAPPA / width) * jnp.dot(yf * yf, jnp.ones((width,), jnp.float32), precision=hi))
    col_basket2 = 2.0 * jnp.dot(yf, basket, precision=hi)
    y_core_t = jnp.concatenate([y_cols, y_cols], axis=1)
    ny_cols = y_cols.shape[0]
    features = jnp.concatenate(
        [yf, yf * yf, jnp.ones((ny_cols, 1), jnp.float32),
         jnp.zeros((ny_cols, KF - 2 * width - 1), jnp.float32)], axis=1
    ).astype(jnp.bfloat16)

    log_col = jnp.log(mass_cols)
    nrows = x_rows.shape[0]

    gshift = col_term2 + pot_cols / EPS + log_col
    row_local = row_lse(q_core, y_core_t, row_basket2, col_basket2, row_term2, gshift)
    nu_part = jnp.sum(mass_cols)
    row_msg = jnp.concatenate([row_local, jnp.stack([nu_part, rmass_part])])
    row_all = gather_col(row_msg[None, :])
    nu_total = jnp.sum(row_all[:, nrows])
    mu_total = jnp.sum(row_all[:, nrows + 1])
    log_nu_total = jnp.log(nu_total)
    row_potential = -EPS * (merge_lse(row_all[:, :nrows]) - log_nu_total)
    fshift = row_term2 + row_potential / EPS + log_row

    col_local = col_lse(q_core, y_core_t, row_basket2, col_basket2, fshift, col_term2)
    col_x = merge_lse(lax.all_gather(col_local, ROW[1], axis=0))
    col_all = lax.all_gather(col_x, ROW[0], axis=0)
    col_potential_new = -EPS * (merge_lse(col_all) - jnp.log(mu_total))
    gq = col_term2 + col_potential_new / EPS + log_col - log_nu_total
    fq = row_term2 + row_potential / EPS

    both = moments(q_core, y_core_t, row_basket2, col_basket2, fq, gq, features)
    both = both[:, : 2 * width + 1]
    own = lax.psum_scatter(both, COL, scatter_dimension=0, tiled=True)
    first = own[:, :width]
    second = own[:, width : 2 * width]
    own_mass = own[:, 2 * width]
    xo = x_points.astype(jnp.float32)
    grad = first - xo * own_mass[:, None]
    curv = (second - 2.0 * xo * first + xo * xo * own_mass[:, None]) / EPS + RIDGE
    multipliers_new = multipliers.astype(jnp.float32) - damping[None, :] * grad / curv
    return (row_potential, col_potential_new, multipliers_new)


def solution(mesh):
    nrow, ncol = mesh.devices.shape
    split = Mesh(mesh.devices.reshape(nrow // 4, 4, ncol // 2, 2), ROW + COL)
    placed = (
        P(ROW + COL, None),
        P(COL + ROW, None),
        P(ROW + COL),
        P(COL + ROW),
        P(ROW + COL, None),
        P(COL + ROW),
        P(),
        P(),
    )
    return jax.shard_map(
        sweep,
        mesh=split,
        in_specs=placed,
        out_specs=(P(ROW), P(COL), P(ROW + COL, None)),
        check_vma=False,
    )
```

```python
import functools

import jax
import jax.numpy as jnp
from jax import lax
from jax.experimental import pallas as pl
from jax.sharding import Mesh, PartitionSpec as P


EPS = 0.5
KAPPA = 0.5
RIDGE = 1.0


ROW = ("z", "x")
COL = ("y", "core")


def gather_row(value):
    inner = lax.all_gather(value, ROW[1], axis=0, tiled=True)
    return lax.all_gather(inner, ROW[0], axis=0, tiled=True)


def gather_col(value):
    inner = lax.all_gather(value, COL[1], axis=0, tiled=True)
    return lax.all_gather(inner, COL[0], axis=0, tiled=True)


KF = 129
INTERPRET = False


def _row_lse_kernel(qa_ref, yat_ref, rb_ref, cb_ref, ra_ref, ca_ref, out_ref, *, tn):
    tm = qa_ref.shape[0]
    n = yat_ref.shape[0]
    qa = qa_ref[...]
    rb = rb_ref[...]
    ra = ra_ref[...]

    def body(k, carry):
        m, l = carry
        j = pl.multiple_of(k * tn, tn)
        s = lax.dot_general(qa, yat_ref[pl.ds(j, tn), :], (((1,), (1,)), ((), ())), preferred_element_type=jnp.float32)
        z = s + ra + ca_ref[:, pl.ds(j, tn)] + jnp.maximum(cb_ref[:, pl.ds(j, tn)] - rb, 0.0)
        m_new = jnp.maximum(m, jnp.max(z, axis=1, keepdims=True))
        l = l * jnp.exp(m - m_new) + jnp.sum(jnp.exp(z - m_new), axis=1, keepdims=True)
        return m_new, l

    m0 = jnp.full((tm, 1), -jnp.inf, jnp.float32)
    l0 = jnp.zeros((tm, 1), jnp.float32)
    m, l = lax.fori_loop(0, n // tn, body, (m0, l0))
    out_ref[...] = m + jnp.log(l)


def row_lse(qa, yat, rb, cb, ra, ca, tm=1024, tn=2048):
    nr, kq = qa.shape
    n = yat.shape[0]
    tm = min(tm, nr)
    tn = min(tn, n)
    return pl.pallas_call(
        functools.partial(_row_lse_kernel, tn=tn),
        grid=(nr // tm,),
        in_specs=[
            pl.BlockSpec((tm, kq), lambda i: (i, 0)),
            pl.BlockSpec((n, kq), lambda i: (0, 0)),
            pl.BlockSpec((tm, 1), lambda i: (i, 0)),
            pl.BlockSpec((1, n), lambda i: (0, 0)),
            pl.BlockSpec((tm, 1), lambda i: (i, 0)),
            pl.BlockSpec((1, n), lambda i: (0, 0)),
        ],
        out_specs=pl.BlockSpec((tm, 1), lambda i: (i, 0)),
        out_shape=jax.ShapeDtypeStruct((nr, 1), jnp.float32),
        interpret=INTERPRET,
    )(qa, yat, rb[:, None], cb[None, :], ra[:, None], ca[None, :])[:, 0]


def _col_lse_kernel(qa_ref, yat_ref, rb_ref, cb_ref, ra_ref, ca_ref, out_ref, *, tm):
    tn = yat_ref.shape[0]
    nr = qa_ref.shape[0]
    yat = yat_ref[...]
    cb = cb_ref[...]
    ca = ca_ref[...]

    def body(k, carry):
        m, l = carry
        i = pl.multiple_of(k * tm, tm)
        s = lax.dot_general(qa_ref[pl.ds(i, tm), :], yat, (((1,), (1,)), ((), ())), preferred_element_type=jnp.float32)
        z = s + ra_ref[pl.ds(i, tm), :] + ca + jnp.maximum(cb - rb_ref[pl.ds(i, tm), :], 0.0)
        m_new = jnp.maximum(m, jnp.max(z, axis=0, keepdims=True))
        l = l * jnp.exp(m - m_new) + jnp.sum(jnp.exp(z - m_new), axis=0, keepdims=True)
        return m_new, l

    m0 = jnp.full((1, tn), -jnp.inf, jnp.float32)
    l0 = jnp.zeros((1, tn), jnp.float32)
    m, l = lax.fori_loop(0, nr // tm, body, (m0, l0))
    out_ref[...] = m + jnp.log(l)


def col_lse(qa, yat, rb, cb, ra, ca, tm=512, tn=1024):
    nr, kq = qa.shape
    n = yat.shape[0]
    tm = min(tm, nr)
    tn = min(tn, n)
    return pl.pallas_call(
        functools.partial(_col_lse_kernel, tm=tm),
        grid=(n // tn,),
        in_specs=[
            pl.BlockSpec((nr, kq), lambda j: (0, 0)),
            pl.BlockSpec((tn, kq), lambda j: (j, 0)),
            pl.BlockSpec((nr, 1), lambda j: (0, 0)),
            pl.BlockSpec((1, tn), lambda j: (0, j)),
            pl.BlockSpec((nr, 1), lambda j: (0, 0)),
            pl.BlockSpec((1, tn), lambda j: (0, j)),
        ],
        out_specs=pl.BlockSpec((1, tn), lambda j: (0, j)),
        out_shape=jax.ShapeDtypeStruct((1, n), jnp.float32),
        interpret=INTERPRET,
    )(qa, yat, rb[:, None], cb[None, :], ra[:, None], ca[None, :])[0]


def _moment_kernel(qa_ref, yat_ref, rb_ref, cb_ref, ra_ref, ca_ref, f_ref, out_ref, *, tn):
    tm = qa_ref.shape[0]
    n = yat_ref.shape[0]
    qa = qa_ref[...]
    rb = rb_ref[...]
    ra = ra_ref[...]

    def body(k, acc):
        j = pl.multiple_of(k * tn, tn)
        s = lax.dot_general(qa, yat_ref[pl.ds(j, tn), :], (((1,), (1,)), ((), ())), preferred_element_type=jnp.float32)
        z = s + ra + ca_ref[:, pl.ds(j, tn)] + jnp.maximum(cb_ref[:, pl.ds(j, tn)] - rb, 0.0)
        plan = jnp.exp(z).astype(jnp.bfloat16)
        return acc + jnp.dot(plan, f_ref[pl.ds(j, tn), :], preferred_element_type=jnp.float32)

    acc = lax.fori_loop(0, n // tn, body, jnp.zeros((tm, f_ref.shape[1]), jnp.float32))
    out_ref[...] = acc


def moments(qa, yat, rb, cb, ra, ca, feats, tm=512, tn=2048):
    nr, kq = qa.shape
    n = yat.shape[0]
    tm = min(tm, nr)
    tn = min(tn, n)
    nf = feats.shape[1]
    return pl.pallas_call(
        functools.partial(_moment_kernel, tn=tn),
        grid=(nr // tm,),
        in_specs=[
            pl.BlockSpec((tm, kq), lambda i: (i, 0)),
            pl.BlockSpec((n, kq), lambda i: (0, 0)),
            pl.BlockSpec((tm, 1), lambda i: (i, 0)),
            pl.BlockSpec((1, n), lambda i: (0, 0)),
            pl.BlockSpec((tm, 1), lambda i: (i, 0)),
            pl.BlockSpec((1, n), lambda i: (0, 0)),
            pl.BlockSpec((n, nf), lambda i: (0, 0)),
        ],
        out_specs=pl.BlockSpec((tm, nf), lambda i: (i, 0)),
        out_shape=jax.ShapeDtypeStruct((nr, nf), jnp.float32),
        interpret=INTERPRET,
    )(qa, yat, rb[:, None], cb[None, :], ra[:, None], ca[None, :], feats)


def merge_lse(parts):
    top = jnp.max(parts, axis=0)
    return top + jnp.log(jnp.sum(jnp.exp(parts - top[None, :]), axis=0))


def sweep(x_points, y_points, row_mass, col_mass, multipliers, col_potential, basket, damping):
    width = x_points.shape[1]
    share = x_points.shape[0]
    x_pack = jnp.concatenate([x_points, multipliers, row_mass[:, None]], axis=1)
    x_rows_pack = lax.all_gather(x_pack, COL, axis=0, tiled=True)
    x_rows = x_rows_pack[:, :width]
    mult_rows = x_rows_pack[:, width : 2 * width]
    mass_rows = x_rows_pack[:, 2 * width]
    ny = y_points.shape[0]
    own_rmass = jnp.zeros((ny,), jnp.bfloat16).at[:share].set(row_mass)
    y_pack = jnp.concatenate(
        [y_points, col_potential[:, None], col_mass[:, None], own_rmass[:, None]], axis=1
    )
    y_cols_pack = gather_row(y_pack)
    y_cols = y_cols_pack[:, :width]
    pot_cols = y_cols_pack[:, width].astype(jnp.float32)
    mass_cols = y_cols_pack[:, width + 1].astype(jnp.float32)
    rmass_part = jnp.sum(y_cols_pack[:, width + 2].astype(jnp.float32))

    xf = x_rows.astype(jnp.float32)
    hf = mult_rows.astype(jnp.float32)
    row_term2 = 2.0 * (-jnp.sum(hf * xf, axis=1) - KAPPA / width * jnp.sum(xf * xf, axis=1))
    row_basket2 = 2.0 * jnp.sum(xf * basket[None, :], axis=1)
    q_core = jnp.concatenate([mult_rows * 2, x_rows * (2.0 * KAPPA / width * 2.0)], axis=1)
    log_row = jnp.log(mass_rows.astype(jnp.float32))
    yf = y_cols.astype(jnp.float32)
    col_term2 = 2.0 * (-(KAPPA / width) * jnp.sum(yf * yf, axis=1))
    col_basket2 = 2.0 * jnp.sum(yf * basket[None, :], axis=1)
    y_core_t = jnp.concatenate([y_cols, y_cols], axis=1)
    ny_cols = y_cols.shape[0]
    features = jnp.concatenate(
        [yf, yf * yf, jnp.ones((ny_cols, 1), jnp.float32),
         jnp.zeros((ny_cols, KF - 2 * width - 1), jnp.float32)], axis=1
    ).astype(jnp.bfloat16)

    log_col = jnp.log(mass_cols)
    nrows = x_rows.shape[0]

    gshift = col_term2 + pot_cols / EPS + log_col
    row_local = row_lse(q_core, y_core_t, row_basket2, col_basket2, row_term2, gshift)
    nu_part = jnp.sum(mass_cols)
    row_msg = jnp.concatenate([row_local, jnp.stack([nu_part, rmass_part])])
    row_all = gather_col(row_msg[None, :])
    nu_total = jnp.sum(row_all[:, nrows])
    mu_total = jnp.sum(row_all[:, nrows + 1])
    log_nu_total = jnp.log(nu_total)
    row_potential = -EPS * (merge_lse(row_all[:, :nrows]) - log_nu_total)
    fshift = row_term2 + row_potential / EPS + log_row

    col_local = col_lse(q_core, y_core_t, row_basket2, col_basket2, fshift, col_term2)
    col_x = merge_lse(lax.all_gather(col_local, ROW[1], axis=0))
    col_all = lax.all_gather(col_x, ROW[0], axis=0)
    col_potential_new = -EPS * (merge_lse(col_all) - jnp.log(mu_total))
    gq = col_term2 + col_potential_new / EPS + log_col - log_nu_total
    fq = row_term2 + row_potential / EPS

    both = moments(q_core, y_core_t, row_basket2, col_basket2, fq, gq, features)
    both = both[:, : 2 * width + 1]
    own = lax.psum_scatter(both, COL, scatter_dimension=0, tiled=True)
    first = own[:, :width]
    second = own[:, width : 2 * width]
    own_mass = own[:, 2 * width]
    xo = x_points.astype(jnp.float32)
    grad = first - xo * own_mass[:, None]
    curv = (second - 2.0 * xo * first + xo * xo * own_mass[:, None]) / EPS + RIDGE
    multipliers_new = multipliers.astype(jnp.float32) - damping[None, :] * grad / curv
    return (row_potential, col_potential_new, multipliers_new)


def solution(mesh):
    nrow, ncol = mesh.devices.shape
    split = Mesh(mesh.devices.reshape(nrow // 4, 4, ncol // 2, 2), ROW + COL)
    placed = (
        P(ROW + COL, None),
        P(COL + ROW, None),
        P(ROW + COL),
        P(COL + ROW),
        P(ROW + COL, None),
        P(COL + ROW),
        P(),
        P(),
    )
    return jax.shard_map(
        sweep,
        mesh=split,
        in_specs=placed,
        out_specs=(P(ROW), P(COL), P(ROW + COL, None)),
        check_vma=False,
    )
```
